256 devices in a mesh: seq: 256 (over y, x, z, core).
Axes of the slice: x: 4, y: 4, z: 8, core: 2. Of those that a mesh axis runs over, the one named last changes fastest.
Arguments:
- tokens: int32 [32768], P('seq'), may hold values from 0 to 4
- mask_flags: int32 [32768], P('seq'), may hold values from 0 to 1, as said below
- hidden_in: bfloat16 [32768, 1280], P('seq'), may hold values from -24 to 24
- grad_above: bfloat16 [32768, 1280], P('seq'), may hold values from -1.25 to 1.25
- w_in: bfloat16 [1280, 640], replicated, may hold values from -0.15625 to 0.15625
- conv_weight: bfloat16 [5, 640, 640], replicated, may hold values from -0.109375 to 0.109375
- w_out: bfloat16 [1280, 640], replicated, may hold values from -0.25 to 0.25
- head_weight: bfloat16 [1280, 6], replicated, may hold values from -0.15625 to 0.15625
Outputs:
- mean_loss: float32 [], replicated
- grad_up: bfloat16 [1280, 640], P('seq')
- grad_down: bfloat16 [1280, 640], P('seq')
The draws below stay inside these ranges and needn't reach their ends.
Inputs may be any that keep to these rules, and one draw needn't show every extreme that they name: `mask_flags`: each flag is 0 or 1; the last position of the context is always masked.
All inputs are finite; a program needn't handle non-finite values.
Results may differ from the reference program's by a relative error of at most 0.009.
Values may be sent and summed in bfloat16 or wider, within the bound.
No kernel may reach another device: no remote copies, remote signals or barrier semaphores. Data moves between devices by JAX's collectives and lax.ppermute only.
A program may use at most 64 MiB of HBM per device.

```python
import jax
import jax.numpy as jnp
from jax import lax

D = 1280
NARROW_CHANNELS = 640
KERNEL_TAPS = 5
VOCAB = 6
DEVICE_ROWS = 128
DILATION_STEP = 512
LEN = 32768


def draw_mask_flags(key, part):
    position = jnp.arange(LEN, dtype=jnp.int32)
    random_draw = jax.random.randint(jax.random.fold_in(key, 17), (LEN,), 0, 5 * LEN, dtype=jnp.int32)
    chosen = (random_draw < LEN // 2 + position) | (position == LEN - 1)
    return chosen.astype(jnp.int32)


def set_ends(values, key, least, top_value):
    dims = values.shape
    place = [jax.random.randint(jax.random.fold_in(key, axis), (), 0, dims[axis]) for axis in range(len(dims))]
    values = values.at[tuple(place)].set(least)
    longest = dims.index(max(dims))
    place[longest] = (place[longest] + 1) % dims[longest]
    return values.at[tuple(place)].set(top_value)


def with_spikes(values, stream_key, source, target, parts, factor):
    owner, partner = [(jnp.arange(values.shape[axis_at]) // (values.shape[axis_at] // parts)).reshape([-1 if axis == axis_at else 1 for axis in range(values.ndim)]) for axis_at in (source, target)]
    chosen = jax.random.permutation(stream_key, parts)[partner]
    strong = (owner == chosen) | (owner == (partner + parts // 2) % parts)
    return jnp.where(strong, factor * values, values)


def levels(rng, dims, split, least, high):
    gain, own = 1.0, jax.random.fold_in(rng, 6)
    for dim, parts in split:
        steps = jnp.exp(jax.random.uniform(jax.random.fold_in(own, dim), (parts,), jnp.float32, least / len(split), high / len(split)))
        gain = gain * jnp.repeat(steps, dims[dim] // parts).reshape([-1 if axis == dim else 1 for axis in range(len(dims))])
    return gain


def bell_draw(key, shape, scale, bound, pieces=(), kind=jnp.bfloat16):
    drawn = jax.random.normal(key, shape, jnp.float32) * scale
    if len(pieces) > 0:
        drawn = levels(key, shape, pieces, -0.22, 0.18) * drawn
    return jnp.clip(drawn, min=-bound, max=bound).astype(kind)


def noise_with(stream_key, dims, deviation, bound, shards, heavy, kind=jnp.bfloat16):
    values = deviation * jax.random.normal(stream_key, dims, jnp.float32)
    if shards:
        values = values * levels(stream_key, dims, shards, -0.22, 0.18)
    return jnp.clip(with_spikes(values, jax.random.fold_in(stream_key, 3), *heavy), -bound, bound).astype(kind)


def setup_inputs(seed: int = 0) -> dict:
    splits = jax.random.split(jax.random.key(seed), 9)
    return {
        "tokens": set_ends(jax.random.randint(splits[0], (LEN,), 0, VOCAB - 1), jax.random.fold_in(splits[0], 1), 0, (VOCAB - 1) - 1).astype(jnp.int32),
        "mask_flags": draw_mask_flags(jax.random.fold_in(splits[8], 71), 0),
        "hidden_in": noise_with(splits[2], (LEN, D), 1.0, 24.0, ((0, 256),), (0, 1, 256, 6.0)),
        "grad_above": noise_with(splits[3], (LEN, D), 0.05, 1.25, ((0, 256),), (0, 1, 256, 6.0)),
        "w_in": bell_draw(splits[4], (D, NARROW_CHANNELS), D ** -0.5, 0.15625),
        "conv_weight": bell_draw(splits[5], (KERNEL_TAPS, NARROW_CHANNELS, NARROW_CHANNELS), (KERNEL_TAPS * NARROW_CHANNELS) ** -0.5, 0.109375),
        "w_out": bell_draw(splits[6], (D, NARROW_CHANNELS), NARROW_CHANNELS ** -0.5, 0.25),
        "head_weight": bell_draw(splits[7], (D, VOCAB), D ** -0.5, 0.15625),
    }


def norm_gelu(values):
    centered = values - lax.optimization_barrier(jnp.mean(values, -1, keepdims=True))
    variance = lax.optimization_barrier(jnp.mean(centered * centered, -1, keepdims=True))
    return jax.nn.gelu(centered * lax.rsqrt(variance + 1e-05))

def first_layer(block_hidden, w_in):
    first_act = norm_gelu(block_hidden.astype(jnp.float32)).astype(jnp.bfloat16)
    first_pre = jnp.dot(first_act, w_in, preferred_element_type=jnp.float32)
    return (first_act, first_pre)

def reference(tokens, mask_flags, hidden_in, grad_above, w_in, conv_weight, w_out, head_weight):
    block_count = LEN // DEVICE_ROWS
    tap_half_count = KERNEL_TAPS // 2
    tok_blocks = tokens.reshape(block_count, DEVICE_ROWS)
    flag_blocks = mask_flags.reshape(block_count, DEVICE_ROWS)
    hidden_blocks = hidden_in.reshape(block_count, DEVICE_ROWS, D)
    above_blocks = grad_above.reshape(block_count, DEVICE_ROWS, D)
    block_index = jnp.arange(block_count, dtype=jnp.int32)
    mask_total = jnp.sum(mask_flags.astype(jnp.float32))
    grad_factor = LEN / mask_total

    def forward_neck(block_hidden):
        first_act, first_pre = first_layer(block_hidden, w_in)
        return norm_gelu(first_pre).astype(jnp.bfloat16)
    narrow_activation = lax.map(forward_neck, hidden_blocks).reshape(LEN, NARROW_CHANNELS)
    empty_border = jnp.zeros((tap_half_count * DILATION_STEP, NARROW_CHANNELS), narrow_activation.dtype)
    narrow_with_border = jnp.concatenate([empty_border, narrow_activation, empty_border], 0)

    def second(carried, inputs_now):
        loss_acc, grad_down = carried
        index_now, block_tokens, block_flags, block_hidden, block_above = inputs_now
        leading_row = (index_now * DEVICE_ROWS).astype(jnp.int32)
        kernel_tap_pile = jnp.stack([lax.dynamic_slice_in_dim(narrow_with_border, leading_row + kernel_tap_index * DILATION_STEP, DEVICE_ROWS, 0) for kernel_tap_index in range(KERNEL_TAPS)])
        conv_pre = jnp.einsum('krc,kcb->rb', kernel_tap_pile.astype(jnp.float32), conv_weight.astype(jnp.float32))
        conv_act = norm_gelu(conv_pre).astype(jnp.bfloat16)
        projected = jnp.dot(conv_act, w_out.T, preferred_element_type=jnp.float32)
        block_out = (block_hidden.astype(jnp.float32) + projected).astype(jnp.bfloat16)
        logits = jnp.dot(block_out, head_weight, preferred_element_type=jnp.float32)
        log_total = jnp.log(lax.optimization_barrier(jnp.sum(jnp.exp(logits), -1)))
        target_hot = (block_tokens[:, None] == jnp.arange(VOCAB, dtype=jnp.int32)[None, :]).astype(jnp.float32)
        cross_ent = log_total - lax.optimization_barrier(jnp.sum(target_hot * logits, -1))
        masked = block_flags.astype(jnp.float32)
        probability = jnp.exp(logits - log_total[:, None])
        grad_logits = (masked[:, None] * (probability - target_hot) * grad_factor).astype(jnp.bfloat16)
        head_part = jnp.dot(grad_logits, head_weight.T, preferred_element_type=jnp.float32)
        grad_block = (head_part + block_above.astype(jnp.float32)).astype(jnp.bfloat16)
        grad_down = grad_down + jnp.dot(grad_block.T, conv_act, preferred_element_type=jnp.float32)
        grad_conv_act = jnp.dot(grad_block, w_out, preferred_element_type=jnp.float32)
        gradient_before_activation = jax.vjp(norm_gelu, conv_pre)[1](grad_conv_act)[0].astype(jnp.bfloat16)
        return ((loss_acc + jnp.sum(masked * cross_ent), grad_down), gradient_before_activation)
    start_carry = (jnp.zeros((), jnp.float32), jnp.zeros((D, NARROW_CHANNELS), jnp.float32))
    (loss_total, grad_down), gradient_before_activation = lax.scan(second, start_carry, (block_index, tok_blocks, flag_blocks, hidden_blocks, above_blocks))
    gradient_before_activation = gradient_before_activation.reshape(LEN, NARROW_CHANNELS)
    empty_gradient = jnp.zeros((tap_half_count * DILATION_STEP, NARROW_CHANNELS), gradient_before_activation.dtype)
    gradient_with_border = jnp.concatenate([empty_gradient, gradient_before_activation, empty_gradient], 0)

    def third(grad_up, inputs_now):
        index_now, block_hidden = inputs_now
        leading_row = (index_now * DEVICE_ROWS).astype(jnp.int32)
        backward_tap_pile = jnp.stack([lax.dynamic_slice_in_dim(gradient_with_border, leading_row + (KERNEL_TAPS - 1 - kernel_tap_index) * DILATION_STEP, DEVICE_ROWS, 0) for kernel_tap_index in range(KERNEL_TAPS)])
        grad_neck = jnp.einsum('krc,kbc->rb', backward_tap_pile.astype(jnp.float32), conv_weight.astype(jnp.float32))
        first_act, first_pre = first_layer(block_hidden, w_in)
        grad_first = jax.vjp(norm_gelu, first_pre)[1](grad_neck)[0].astype(jnp.bfloat16)
        return (grad_up + jnp.dot(first_act.T, grad_first, preferred_element_type=jnp.float32), None)
    grad_up, unused = lax.scan(third, jnp.zeros((D, NARROW_CHANNELS), jnp.float32), (block_index, hidden_blocks))
    return (loss_total / mask_total, grad_up.astype(jnp.bfloat16), grad_down.astype(jnp.bfloat16))
```

```python
import jax
import jax.numpy as jnp
from jax import lax
from jax.sharding import PartitionSpec as P


def from_behind(block, axis, distance):
    devices = range(lax.axis_size(axis))
    route = [(i - distance, i) for i in devices if i - distance in devices]
    return lax.ppermute(block, axis, route)


def norm_gelu(values):
    centered = values - jnp.mean(values, -1, keepdims=True)
    variance = jnp.mean(centered * centered, -1, keepdims=True)
    return jax.nn.gelu(centered * lax.rsqrt(variance + 1e-05))


def spread(source_field, shard_reach):
    near_pieces = {}
    far_pieces = {}
    for direction in (1, -1):
        near_pieces[direction] = from_behind(source_field, "seq", direction * shard_reach)
    for direction in (1, -1):
        far_pieces[direction] = from_behind(source_field, "seq", 2 * direction * shard_reach)
    return [far_pieces[1], near_pieces[1], source_field, near_pieces[-1], far_pieces[-1]]


def own_rows(summed, axis):
    devices = lax.axis_size(axis)
    share = summed.shape[0] // devices
    return lax.dynamic_slice_in_dim(summed, lax.axis_index(axis) * share, share, 0)


def shards(tokens, mask_flags, hidden_in, grad_above, w_in, conv_weight, w_out, head_weight):
    local_rows = tokens.shape[0]
    vocab_size = head_weight.shape[1]
    seq_devices = lax.axis_size("seq")
    shard_reach = 4
    context_rows = float(local_rows * seq_devices)
    masked = mask_flags.astype(jnp.float32)
    local_count = jnp.sum(masked)
    count_tile = jnp.broadcast_to(local_count, (256, 128))
    count_summed = lax.psum(count_tile, "seq")
    alphabet = jnp.arange(vocab_size, dtype=jnp.int32)
    first_act = norm_gelu(hidden_in.astype(jnp.float32)).astype(jnp.bfloat16)
    first_pre = jnp.dot(first_act, w_in, preferred_element_type=jnp.float32)
    narrow_activation = norm_gelu(first_pre).astype(jnp.bfloat16)
    kernel_tap_pile = jnp.stack(spread(narrow_activation, shard_reach))
    count_summed, kernel_tap_pile = lax.optimization_barrier((count_summed, kernel_tap_pile))
    mask_total = count_summed[0, 0]
    conv_pre = jnp.einsum(
        "krc,kcb->rb", kernel_tap_pile, conv_weight, preferred_element_type=jnp.float32
    )
    conv_act = norm_gelu(conv_pre).astype(jnp.bfloat16)
    projected = lax.dot_general(
        conv_act, w_out, (((1,), (1,)), ((), ())), preferred_element_type=jnp.float32
    )
    block_out = (hidden_in.astype(jnp.float32) + projected).astype(jnp.bfloat16)
    logits_t = lax.dot_general(
        head_weight, block_out, (((0,), (1,)), ((), ())), preferred_element_type=jnp.float32
    )
    log_total = jnp.log(jnp.sum(jnp.exp(logits_t), 0))
    target_hot = (alphabet[:, None] == tokens[None, :]).astype(jnp.float32)
    cross_ent = log_total - jnp.sum(target_hot * logits_t, 0)
    local_loss = jnp.sum(masked * cross_ent)
    probability = jnp.exp(logits_t - log_total[None, :])
    grad_logits = (
        masked[None, :] * (probability - target_hot) * (context_rows / mask_total)
    ).astype(jnp.bfloat16)
    head_part = lax.dot_general(
        grad_logits, head_weight, (((0,), (1,)), ((), ())), preferred_element_type=jnp.float32
    )
    grad_block = (head_part + grad_above.astype(jnp.float32)).astype(jnp.bfloat16)
    columns = grad_block
    down_partial = lax.dot_general(
        columns, conv_act, (((0,), (0,)), ((), ())), preferred_element_type=jnp.float32
    )
    loss_rows = jnp.broadcast_to(local_loss, (8, down_partial.shape[1]))
    grad_conv_act = jnp.dot(grad_block, w_out, preferred_element_type=jnp.float32)
    gradient_before_activation = jax.vjp(norm_gelu, conv_pre)[1](grad_conv_act)[0].astype(
        jnp.bfloat16
    )
    back_pieces = spread(gradient_before_activation, shard_reach)
    backward_tap_pile = jnp.stack(back_pieces[::-1])
    grad_neck = jnp.einsum(
        "krc,kbc->rb", backward_tap_pile, conv_weight, preferred_element_type=jnp.float32
    )
    grad_first = jax.vjp(norm_gelu, first_pre)[1](grad_neck)[0].astype(jnp.bfloat16)
    columns = first_act
    up_partial = lax.dot_general(
        columns, grad_first, (((0,), (0,)), ((), ())), preferred_element_type=jnp.float32
    )
    width = down_partial.shape[0]
    summed = lax.psum(jnp.concatenate([down_partial, up_partial, loss_rows], 0), "seq")
    loss_total = summed[-1, 0]
    grad_down = own_rows(summed[:width], "seq").astype(jnp.bfloat16)
    grad_up = own_rows(summed[width : 2 * width], "seq").astype(jnp.bfloat16)
    return (loss_total / mask_total, grad_up, grad_down)


def solution(mesh):
    placed = (P("seq"), P("seq"), P("seq", None), P("seq", None), P(), P(), P(), P())
    return jax.shard_map(
        shards,
        mesh=mesh,
        in_specs=placed,
        out_specs=(P(), P("seq", None), P("seq", None)),
        check_vma=False,
    )
```

```python
import jax
import jax.numpy as jnp
from jax import lax
from jax.sharding import PartitionSpec as P


def from_behind(block, axis, distance):
    devices = range(lax.axis_size(axis))
    route = [(i - distance, i) for i in devices if i - distance in devices]
    return lax.ppermute(block, axis, route)


def swap_with(block, axis, bit):
    devices = lax.axis_size(axis)
    return lax.ppermute(block, axis, [(i, i ^ bit) for i in range(devices)])


def link_order(devices):
    bits = [1 << k for k in range(devices.bit_length() - 1)]
    near = [1, 2, 16, 64, 4, 32, 128, 8]
    return [b for b in near if b in bits] + [b for b in bits if b not in near]


def tree_sum(values, axis):
    for bit in link_order(lax.axis_size(axis)):
        values = values + swap_with(values, axis, bit)
    return values


def tree_scatter(partial, axis):
    devices = lax.axis_size(axis)
    depth = devices.bit_length() - 1
    me = lax.axis_index(axis)
    rows, cols = partial.shape
    blocks = partial.reshape((2,) * depth + (rows // devices, cols))
    dim_bits = [1 << (depth - 1 - d) for d in range(depth)]
    for bit in link_order(devices):
        at = dim_bits.index(bit)
        upper = (me & bit) != 0
        low = lax.index_in_dim(blocks, 0, at, keepdims=False)
        high = lax.index_in_dim(blocks, 1, at, keepdims=False)
        keep = jnp.where(upper, high, low)
        send = jnp.where(upper, low, high).astype(jnp.bfloat16)
        blocks = keep + swap_with(send, axis, bit).astype(jnp.float32)
        dim_bits.pop(at)
    return blocks


def norm_gelu(values):
    centered = values - jnp.mean(values, -1, keepdims=True)
    variance = jnp.mean(centered * centered, -1, keepdims=True)
    return jax.nn.gelu(centered * lax.rsqrt(variance + 1e-05))


def spread(source_field, shard_reach):
    near_pieces = {}
    far_pieces = {}
    for direction in (1, -1):
        near_pieces[direction] = from_behind(source_field, "seq", direction * shard_reach)
    for direction in (1, -1):
        far_pieces[direction] = from_behind(source_field, "seq", 2 * direction * shard_reach)
    return [far_pieces[1], near_pieces[1], source_field, near_pieces[-1], far_pieces[-1]]


def shards(tokens, mask_flags, hidden_in, grad_above, w_in, conv_weight, w_out, head_weight):
    local_rows = tokens.shape[0]
    vocab_size = head_weight.shape[1]
    seq_devices = lax.axis_size("seq")
    shard_reach = 4
    context_rows = float(local_rows * seq_devices)
    masked = mask_flags.astype(jnp.float32)
    local_count = jnp.sum(masked)
    mask_total = tree_sum(jnp.broadcast_to(local_count, (8, 128)), "seq")[0, 0]
    alphabet = jnp.arange(vocab_size, dtype=jnp.int32)
    first_act = norm_gelu(hidden_in.astype(jnp.float32)).astype(jnp.bfloat16)
    first_pre = jnp.dot(first_act, w_in, preferred_element_type=jnp.float32)
    narrow_activation = norm_gelu(first_pre).astype(jnp.bfloat16)
    kernel_tap_pile = jnp.stack(spread(narrow_activation, shard_reach))
    conv_pre = jnp.einsum(
        "krc,kcb->rb", kernel_tap_pile, conv_weight, preferred_element_type=jnp.float32
    )
    conv_act = norm_gelu(conv_pre).astype(jnp.bfloat16)
    projected = lax.dot_general(
        conv_act, w_out, (((1,), (1,)), ((), ())), preferred_element_type=jnp.float32
    )
    block_out = (hidden_in.astype(jnp.float32) + projected).astype(jnp.bfloat16)
    logits_t = lax.dot_general(
        head_weight, block_out, (((0,), (1,)), ((), ())), preferred_element_type=jnp.float32
    )
    log_total = jnp.log(jnp.sum(jnp.exp(logits_t), 0))
    target_hot = (alphabet[:, None] == tokens[None, :]).astype(jnp.float32)
    cross_ent = log_total - jnp.sum(target_hot * logits_t, 0)
    local_loss = jnp.sum(masked * cross_ent)
    probability = jnp.exp(logits_t - log_total[None, :])
    grad_logits = (
        masked[None, :] * (probability - target_hot) * (context_rows / mask_total)
    ).astype(jnp.bfloat16)
    head_part = lax.dot_general(
        grad_logits, head_weight, (((0,), (1,)), ((), ())), preferred_element_type=jnp.float32
    )
    grad_block = (head_part + grad_above.astype(jnp.float32)).astype(jnp.bfloat16)
    columns = grad_block
    grad_down = tree_scatter(
        lax.dot_general(
            columns, conv_act, (((0,), (0,)), ((), ())), preferred_element_type=jnp.float32
        ),
        "seq",
    ).astype(jnp.bfloat16)
    grad_conv_act = jnp.dot(grad_block, w_out, preferred_element_type=jnp.float32)
    gradient_before_activation = jax.vjp(norm_gelu, conv_pre)[1](grad_conv_act)[0].astype(
        jnp.bfloat16
    )
    back_pieces = spread(gradient_before_activation, shard_reach)
    backward_tap_pile = jnp.stack(back_pieces[::-1])
    grad_neck = jnp.einsum(
        "krc,kbc->rb", backward_tap_pile, conv_weight, preferred_element_type=jnp.float32
    )
    grad_first = jax.vjp(norm_gelu, first_pre)[1](grad_neck)[0].astype(jnp.bfloat16)
    columns = first_act
    grad_up = tree_scatter(
        lax.dot_general(
            columns, grad_first, (((0,), (0,)), ((), ())), preferred_element_type=jnp.float32
        ),
        "seq",
    ).astype(jnp.bfloat16)
    loss_total = tree_sum(jnp.broadcast_to(local_loss, (8, 128)), "seq")[0, 0]
    return (loss_total / mask_total, grad_up, grad_down)


def solution(mesh):
    placed = (P("seq"), P("seq"), P("seq", None), P("seq", None), P(), P(), P(), P())
    return jax.shard_map(
        shards,
        mesh=mesh,
        in_specs=placed,
        out_specs=(P(), P("seq", None), P("seq", None)),
        check_vma=False,
    )
```

```python
import jax
import jax.numpy as jnp
from jax import lax
from jax.sharding import PartitionSpec as P


def from_behind(block, axis, distance):
    devices = range(lax.axis_size(axis))
    route = [(i - distance, i) for i in devices if i - distance in devices]
    return lax.ppermute(block, axis, route)


def swap_with(block, axis, bit):
    devices = lax.axis_size(axis)
    return lax.ppermute(block, axis, [(i, i ^ bit) for i in range(devices)])


def link_order(devices):
    bits = [1 << k for k in range(devices.bit_length() - 1)]
    near = [1, 2, 16, 64, 4, 32, 128, 8]
    return [b for b in near if b in bits] + [b for b in bits if b not in near]


def tree_sum(values, axis):
    for bit in link_order(lax.axis_size(axis)):
        values = values + swap_with(values, axis, bit)
    return values


def tree_scatter(partial, extra, axis):
    devices = lax.axis_size(axis)
    depth = devices.bit_length() - 1
    me = lax.axis_index(axis)
    blocks = partial.reshape((2,) * depth + partial.shape[1:])
    dim_bits = [1 << (depth - 1 - d) for d in range(depth)]
    for bit in link_order(devices):
        at = dim_bits.index(bit)
        upper = (me & bit) != 0
        low = lax.index_in_dim(blocks, 0, at, keepdims=False)
        high = lax.index_in_dim(blocks, 1, at, keepdims=False)
        keep = jnp.where(upper, high, low)
        send = jnp.where(upper, low, high).astype(jnp.bfloat16)
        got, got_extra = swap_with((send, extra), axis, bit)
        blocks = keep + got.astype(jnp.float32)
        extra = extra + got_extra
        dim_bits.pop(at)
    return blocks, extra


def norm_gelu(values):
    centered = values - jnp.mean(values, -1, keepdims=True)
    variance = jnp.mean(centered * centered, -1, keepdims=True)
    return jax.nn.gelu(centered * lax.rsqrt(variance + 1e-05))


def spread(source_field, shard_reach):
    near_pieces = {}
    far_pieces = {}
    for direction in (1, -1):
        near_pieces[direction] = from_behind(source_field, "seq", direction * shard_reach)
    for direction in (1, -1):
        far_pieces[direction] = from_behind(source_field, "seq", 2 * direction * shard_reach)
    return [far_pieces[1], near_pieces[1], source_field, near_pieces[-1], far_pieces[-1]]


def shards(tokens, mask_flags, hidden_in, grad_above, w_in, conv_weight, w_out, head_weight):
    local_rows = tokens.shape[0]
    vocab_size = head_weight.shape[1]
    seq_devices = lax.axis_size("seq")
    shard_reach = 4
    context_rows = float(local_rows * seq_devices)
    masked = mask_flags.astype(jnp.float32)
    local_count = jnp.sum(masked)
    mask_total = tree_sum(jnp.broadcast_to(local_count, (8, 128)), "seq")[0, 0]
    alphabet = jnp.arange(vocab_size, dtype=jnp.int32)
    first_act = norm_gelu(hidden_in.astype(jnp.float32)).astype(jnp.bfloat16)
    first_pre = jnp.dot(first_act, w_in, preferred_element_type=jnp.float32)
    narrow_activation = norm_gelu(first_pre).astype(jnp.bfloat16)
    kernel_tap_pile = jnp.stack(spread(narrow_activation, shard_reach))
    conv_pre = jnp.einsum(
        "krc,kcb->rb", kernel_tap_pile, conv_weight, preferred_element_type=jnp.float32
    )
    conv_act = norm_gelu(conv_pre).astype(jnp.bfloat16)
    projected = lax.dot_general(
        conv_act, w_out, (((1,), (1,)), ((), ())), preferred_element_type=jnp.float32
    )
    block_out = (hidden_in.astype(jnp.float32) + projected).astype(jnp.bfloat16)
    logits_t = lax.dot_general(
        head_weight, block_out, (((0,), (1,)), ((), ())), preferred_element_type=jnp.float32
    )
    log_total = jnp.log(jnp.sum(jnp.exp(logits_t), 0))
    target_hot = (alphabet[:, None] == tokens[None, :]).astype(jnp.float32)
    cross_ent = log_total - jnp.sum(target_hot * logits_t, 0)
    local_loss = jnp.sum(masked * cross_ent)
    probability = jnp.exp(logits_t - log_total[None, :])
    grad_logits = (
        masked[None, :] * (probability - target_hot) * (context_rows / mask_total)
    ).astype(jnp.bfloat16)
    head_part = lax.dot_general(
        grad_logits, head_weight, (((0,), (1,)), ((), ())), preferred_element_type=jnp.float32
    )
    grad_block = (head_part + grad_above.astype(jnp.float32)).astype(jnp.bfloat16)
    columns = grad_block
    down_partial = lax.dot_general(
        columns, conv_act, (((0,), (0,)), ((), ())), preferred_element_type=jnp.float32
    )
    grad_conv_act = jnp.dot(grad_block, w_out, preferred_element_type=jnp.float32)
    gradient_before_activation = jax.vjp(norm_gelu, conv_pre)[1](grad_conv_act)[0].astype(
        jnp.bfloat16
    )
    back_pieces = spread(gradient_before_activation, shard_reach)
    backward_tap_pile = jnp.stack(back_pieces[::-1])
    grad_neck = jnp.einsum(
        "krc,kbc->rb", backward_tap_pile, conv_weight, preferred_element_type=jnp.float32
    )
    grad_first = jax.vjp(norm_gelu, first_pre)[1](grad_neck)[0].astype(jnp.bfloat16)
    columns = first_act
    up_partial = lax.dot_general(
        columns, grad_first, (((0,), (0,)), ((), ())), preferred_element_type=jnp.float32
    )
    share = up_partial.shape[0] // seq_devices
    both = jnp.concatenate(
        [
            down_partial.reshape(seq_devices, share, -1),
            up_partial.reshape(seq_devices, share, -1),
        ],
        1,
    )
    mine, loss_tile = tree_scatter(both, jnp.broadcast_to(local_loss, (8, 128)), "seq")
    grad_down = mine[:share].astype(jnp.bfloat16)
    grad_up = mine[share:].astype(jnp.bfloat16)
    loss_total = loss_tile[0, 0]
    return (loss_total / mask_total, grad_up, grad_down)


def solution(mesh):
    placed = (P("seq"), P("seq"), P("seq", None), P("seq", None), P(), P(), P(), P())
    return jax.shard_map(
        shards,
        mesh=mesh,
        in_specs=placed,
        out_specs=(P(), P("seq", None), P("seq", None)),
        check_vma=False,
    )
```

```python
import jax
import jax.numpy as jnp
from jax import lax
from jax.sharding import PartitionSpec as P


def from_behind(block, axis, distance):
    devices = range(lax.axis_size(axis))
    route = [(i - distance, i) for i in devices if i - distance in devices]
    return lax.ppermute(block, axis, route)


def swap_with(block, axis, bit):
    devices = lax.axis_size(axis)
    return lax.ppermute(block, axis, [(i, i ^ bit) for i in range(devices)])


def link_order(devices):
    bits = [1 << k for k in range(devices.bit_length() - 1)]
    near = [1, 2, 16, 64, 4, 32, 128, 8]
    return [b for b in near if b in bits] + [b for b in bits if b not in near]


def tree_sum(values, axis):
    for bit in link_order(lax.axis_size(axis)):
        values = values + swap_with(values, axis, bit)
    return values


def count_sum(counts, axis):
    order = link_order(lax.axis_size(axis))
    for first, second in zip(order[0::2], order[1::2]):
        counts = (
            counts
            + swap_with(counts, axis, first)
            + swap_with(counts, axis, second)
            + swap_with(counts, axis, first ^ second)
        )
    return counts


def tree_layout(columns, axis):
    devices = lax.axis_size(axis)
    depth = devices.bit_length() - 1
    rows, width = columns.shape
    split = columns.reshape((rows,) + (2,) * depth + (width // devices,))
    axes = [1 + depth - 1 - (bit.bit_length() - 1) for bit in link_order(devices)]
    return split.transpose([0] + axes + [depth + 1]).reshape(rows, width)


def tree_scatter(partials, extra, axis):
    devices = lax.axis_size(axis)
    me = lax.axis_index(axis)
    blocks = [p.reshape(devices, p.shape[0] // devices, -1) for p in partials]
    for bit in link_order(devices):
        half = blocks[0].shape[0] // 2
        upper = (me // bit) % 2
        keep = [lax.dynamic_slice_in_dim(b, upper * half, half, 0) for b in blocks]
        send = [
            lax.dynamic_slice_in_dim(b, (1 - upper) * half, half, 0).astype(jnp.bfloat16)
            for b in blocks
        ]
        got, got_extra = swap_with((send, extra), axis, bit)
        blocks = [k + g.astype(jnp.float32) for k, g in zip(keep, got)]
        extra = extra + got_extra
    return [b[0] for b in blocks], extra


def norm_gelu(values):
    centered = values - jnp.mean(values, -1, keepdims=True)
    variance = jnp.mean(centered * centered, -1, keepdims=True)
    return jax.nn.gelu(centered * lax.rsqrt(variance + 1e-05))


def spread(source_field, shard_reach):
    near_pieces = {}
    far_pieces = {}
    for direction in (1, -1):
        near_pieces[direction] = from_behind(source_field, "seq", direction * shard_reach)
    for direction in (1, -1):
        far_pieces[direction] = from_behind(source_field, "seq", 2 * direction * shard_reach)
    return [far_pieces[1], near_pieces[1], source_field, near_pieces[-1], far_pieces[-1]]


def shards(tokens, mask_flags, hidden_in, grad_above, w_in, conv_weight, w_out, head_weight):
    local_rows = tokens.shape[0]
    vocab_size = head_weight.shape[1]
    seq_devices = lax.axis_size("seq")
    shard_reach = 4
    context_rows = float(local_rows * seq_devices)
    masked = mask_flags.astype(jnp.float32)
    local_count = jnp.sum(masked)
    mask_total = count_sum(jnp.broadcast_to(local_count, (8, 128)), "seq")[0, 0]
    alphabet = jnp.arange(vocab_size, dtype=jnp.int32)
    first_act = norm_gelu(hidden_in.astype(jnp.float32)).astype(jnp.bfloat16)
    first_pre = jnp.dot(first_act, w_in, preferred_element_type=jnp.float32)
    narrow_activation = norm_gelu(first_pre).astype(jnp.bfloat16)
    kernel_tap_pile = jnp.stack(spread(narrow_activation, shard_reach))
    conv_pre = jnp.einsum(
        "krc,kcb->rb", kernel_tap_pile, conv_weight, preferred_element_type=jnp.float32
    )
    conv_act = norm_gelu(conv_pre).astype(jnp.bfloat16)
    projected = lax.dot_general(
        conv_act, w_out, (((1,), (1,)), ((), ())), preferred_element_type=jnp.float32
    )
    block_out = (hidden_in.astype(jnp.float32) + projected).astype(jnp.bfloat16)
    logits_t = lax.dot_general(
        head_weight, block_out, (((0,), (1,)), ((), ())), preferred_element_type=jnp.float32
    )
    log_total = jnp.log(jnp.sum(jnp.exp(logits_t), 0))
    target_hot = (alphabet[:, None] == tokens[None, :]).astype(jnp.float32)
    cross_ent = log_total - jnp.sum(target_hot * logits_t, 0)
    local_loss = jnp.sum(masked * cross_ent)
    probability = jnp.exp(logits_t - log_total[None, :])
    grad_logits = (
        masked[None, :] * (probability - target_hot) * (context_rows / mask_total)
    ).astype(jnp.bfloat16)
    head_part = lax.dot_general(
        grad_logits, head_weight, (((0,), (1,)), ((), ())), preferred_element_type=jnp.float32
    )
    grad_block = (head_part + grad_above.astype(jnp.float32)).astype(jnp.bfloat16)
    columns = tree_layout(grad_block, "seq")
    down_partial = lax.dot_general(
        columns, conv_act, (((0,), (0,)), ((), ())), preferred_element_type=jnp.float32
    )
    grad_conv_act = jnp.dot(grad_block, w_out, preferred_element_type=jnp.float32)
    gradient_before_activation = jax.vjp(norm_gelu, conv_pre)[1](grad_conv_act)[0].astype(
        jnp.bfloat16
    )
    back_pieces = spread(gradient_before_activation, shard_reach)
    backward_tap_pile = jnp.stack(back_pieces[::-1])
    grad_neck = jnp.einsum(
        "krc,kbc->rb", backward_tap_pile, conv_weight, preferred_element_type=jnp.float32
    )
    grad_first = jax.vjp(norm_gelu, first_pre)[1](grad_neck)[0].astype(jnp.bfloat16)
    columns = tree_layout(first_act, "seq")
    up_partial = lax.dot_general(
        columns, grad_first, (((0,), (0,)), ((), ())), preferred_element_type=jnp.float32
    )
    (grad_down, grad_up), loss_tile = tree_scatter(
        (down_partial, up_partial), jnp.broadcast_to(local_loss, (8, 128)), "seq"
    )
    grad_down = grad_down.astype(jnp.bfloat16)
    grad_up = grad_up.astype(jnp.bfloat16)
    loss_total = loss_tile[0, 0]
    return (loss_total / mask_total, grad_up, grad_down)


def solution(mesh):
    placed = (P("seq"), P("seq"), P("seq", None), P("seq", None), P(), P(), P(), P())
    return jax.shard_map(
        shards,
        mesh=mesh,
        in_specs=placed,
        out_specs=(P(), P("seq", None), P("seq", None)),
        check_vma=False,
    )
```

```python
import jax
import jax.numpy as jnp
from jax import lax
from jax.sharding import PartitionSpec as P


def from_behind(block, axis, distance):
    devices = range(lax.axis_size(axis))
    route = [(i - distance, i) for i in devices if i - distance in devices]
    return lax.ppermute(block, axis, route)


def swap_with(block, axis, bit):
    devices = lax.axis_size(axis)
    return lax.ppermute(block, axis, [(i, i ^ bit) for i in range(devices)])


def link_order(devices):
    bits = [1 << k for k in range(devices.bit_length() - 1)]
    near = [1, 2, 16, 64, 4, 32, 128, 8]
    return [b for b in near if b in bits] + [b for b in bits if b not in near]


def tree_sum(values, axis):
    for bit in link_order(lax.axis_size(axis)):
        values = values + swap_with(values, axis, bit)
    return values


def count_sum(counts, axis):
    order = link_order(lax.axis_size(axis))
    for first, second in zip(order[0::2], order[1::2]):
        counts = (
            counts
            + swap_with(counts, axis, first)
            + swap_with(counts, axis, second)
            + swap_with(counts, axis, first ^ second)
        )
    return counts


def tree_layout(columns, axis):
    devices = lax.axis_size(axis)
    depth = devices.bit_length() - 1
    rows, width = columns.shape
    split = columns.reshape((rows,) + (2,) * depth + (width // devices,))
    axes = [1 + depth - 1 - (bit.bit_length() - 1) for bit in link_order(devices)]
    return split.transpose([0] + axes + [depth + 1]).reshape(rows, width)


def split_pair(value):
    high = value.astype(jnp.bfloat16)
    low = (value - high.astype(jnp.float32)).astype(jnp.bfloat16)
    return high, low


def tree_scatter(partials, extra, axis):
    devices = lax.axis_size(axis)
    me = lax.axis_index(axis)
    blocks = [p.reshape(devices, p.shape[0] // devices, -1) for p in partials]
    share, width = blocks[0].shape[1:]
    for bit in link_order(devices):
        half = blocks[0].shape[0] // 2
        upper = (me // bit) % 2
        keep = [lax.dynamic_slice_in_dim(b, upper * half, half, 0) for b in blocks]
        high, low = split_pair(extra)
        extra = high.astype(jnp.float32) + low.astype(jnp.float32)
        tail = jnp.concatenate(
            [jnp.broadcast_to(high, (half, 1, width // 2)), jnp.broadcast_to(low, (half, 1, width // 2))],
            2,
        )
        send = [
            lax.dynamic_slice_in_dim(b, (1 - upper) * half, half, 0).astype(jnp.bfloat16)
            for b in blocks
        ]
        got = swap_with(jnp.concatenate(send + [tail], 1), axis, bit)
        blocks = [
            k + got[:, i * share : (i + 1) * share].astype(jnp.float32) for i, k in enumerate(keep)
        ]
        got_tail = got[0, -1].astype(jnp.float32)
        extra = extra + (got_tail[0] + got_tail[width // 2])
    return [b[0] for b in blocks], extra


def norm_gelu(values):
    centered = values - jnp.mean(values, -1, keepdims=True)
    variance = jnp.mean(centered * centered, -1, keepdims=True)
    return jax.nn.gelu(centered * lax.rsqrt(variance + 1e-05))


def spread(source_field, shard_reach):
    near_pieces = {}
    far_pieces = {}
    for direction in (1, -1):
        near_pieces[direction] = from_behind(source_field, "seq", direction * shard_reach)
    for direction in (1, -1):
        far_pieces[direction] = from_behind(source_field, "seq", 2 * direction * shard_reach)
    return [far_pieces[1], near_pieces[1], source_field, near_pieces[-1], far_pieces[-1]]


def shards(tokens, mask_flags, hidden_in, grad_above, w_in, conv_weight, w_out, head_weight):
    local_rows = tokens.shape[0]
    vocab_size = head_weight.shape[1]
    seq_devices = lax.axis_size("seq")
    shard_reach = 4
    context_rows = float(local_rows * seq_devices)
    masked = mask_flags.astype(jnp.float32)
    local_count = jnp.sum(masked)
    mask_total = count_sum(jnp.broadcast_to(local_count, (8, 128)), "seq")[0, 0]
    alphabet = jnp.arange(vocab_size, dtype=jnp.int32)
    first_act = norm_gelu(hidden_in.astype(jnp.float32)).astype(jnp.bfloat16)
    first_pre = jnp.dot(first_act, w_in, preferred_element_type=jnp.float32)
    narrow_activation = norm_gelu(first_pre).astype(jnp.bfloat16)
    kernel_tap_pile = jnp.stack(spread(narrow_activation, shard_reach))
    conv_pre = jnp.einsum(
        "krc,kcb->rb", kernel_tap_pile, conv_weight, preferred_element_type=jnp.float32
    )
    conv_act = norm_gelu(conv_pre).astype(jnp.bfloat16)
    projected = lax.dot_general(
        conv_act, w_out, (((1,), (1,)), ((), ())), preferred_element_type=jnp.float32
    )
    block_out = (hidden_in.astype(jnp.float32) + projected).astype(jnp.bfloat16)
    logits_t = lax.dot_general(
        head_weight, block_out, (((0,), (1,)), ((), ())), preferred_element_type=jnp.float32
    )
    log_total = jnp.log(jnp.sum(jnp.exp(logits_t), 0))
    target_hot = (alphabet[:, None] == tokens[None, :]).astype(jnp.float32)
    cross_ent = log_total - jnp.sum(target_hot * logits_t, 0)
    local_loss = jnp.sum(masked * cross_ent)
    probability = jnp.exp(logits_t - log_total[None, :])
    grad_logits = (
        masked[None, :] * (probability - target_hot) * (context_rows / mask_total)
    ).astype(jnp.bfloat16)
    head_part = lax.dot_general(
        grad_logits, head_weight, (((0,), (1,)), ((), ())), preferred_element_type=jnp.float32
    )
    grad_block = (head_part + grad_above.astype(jnp.float32)).astype(jnp.bfloat16)
    columns = tree_layout(grad_block, "seq")
    down_partial = lax.dot_general(
        columns, conv_act, (((0,), (0,)), ((), ())), preferred_element_type=jnp.float32
    )
    grad_conv_act = jnp.dot(grad_block, w_out, preferred_element_type=jnp.float32)
    gradient_before_activation = jax.vjp(norm_gelu, conv_pre)[1](grad_conv_act)[0].astype(
        jnp.bfloat16
    )
    back_pieces = spread(gradient_before_activation, shard_reach)
    backward_tap_pile = jnp.stack(back_pieces[::-1])
    grad_neck = jnp.einsum(
        "krc,kbc->rb", backward_tap_pile, conv_weight, preferred_element_type=jnp.float32
    )
    grad_first = jax.vjp(norm_gelu, first_pre)[1](grad_neck)[0].astype(jnp.bfloat16)
    columns = tree_layout(first_act, "seq")
    up_partial = lax.dot_general(
        columns, grad_first, (((0,), (0,)), ((), ())), preferred_element_type=jnp.float32
    )
    (grad_down, grad_up), loss_total = tree_scatter((down_partial, up_partial), local_loss, "seq")
    grad_down = grad_down.astype(jnp.bfloat16)
    grad_up = grad_up.astype(jnp.bfloat16)
    return (loss_total / mask_total, grad_up, grad_down)


def solution(mesh):
    placed = (P("seq"), P("seq"), P("seq", None), P("seq", None), P(), P(), P(), P())
    return jax.shard_map(
        shards,
        mesh=mesh,
        in_specs=placed,
        out_specs=(P(), P("seq", None), P("seq", None)),
        check_vma=False,
    )
```

```python
import jax
import jax.numpy as jnp
from jax import lax
from jax.sharding import PartitionSpec as P


def from_behind(block, axis, distance):
    devices = range(lax.axis_size(axis))
    route = [(i - distance, i) for i in devices if i - distance in devices]
    return lax.ppermute(block, axis, route)


def swap_with(block, axis, bit):
    devices = lax.axis_size(axis)
    return lax.ppermute(block, axis, [(i, i ^ bit) for i in range(devices)])


def link_order(devices):
    bits = [1 << k for k in range(devices.bit_length() - 1)]
    near = [1, 2, 16, 64, 4, 32, 128, 8]
    return [b for b in near if b in bits] + [b for b in bits if b not in near]


def tree_sum(values, axis):
    for bit in link_order(lax.axis_size(axis)):
        values = values + swap_with(values, axis, bit)
    return values


def count_sum(counts, axis):
    order = link_order(lax.axis_size(axis))
    for first, second in zip(order[0::2], order[1::2]):
        counts = (
            counts
            + swap_with(counts, axis, first)
            + swap_with(counts, axis, second)
            + swap_with(counts, axis, first ^ second)
        )
    return counts


def tree_layout(columns, axis):
    devices = lax.axis_size(axis)
    depth = devices.bit_length() - 1
    rows, width = columns.shape
    split = columns.reshape((rows,) + (2,) * depth + (width // devices,))
    axes = [1 + depth - 1 - (bit.bit_length() - 1) for bit in link_order(devices)]
    return split.transpose([0] + axes + [depth + 1]).reshape(rows, width)


def tree_scatter(partials, extra, axis):
    devices = lax.axis_size(axis)
    me = lax.axis_index(axis)
    blocks = [p.reshape(devices, p.shape[0] // devices, -1) for p in partials]
    for bit in link_order(devices):
        half = blocks[0].shape[0] // 2
        upper = (me // bit) % 2
        keep = [lax.dynamic_slice_in_dim(b, upper * half, half, 0) for b in blocks]
        send = [
            lax.dynamic_slice_in_dim(b, (1 - upper) * half, half, 0).astype(jnp.bfloat16)
            for b in blocks
        ]
        pieces = 2 if half >= 16 else 1
        parts = [jnp.split(s, pieces, 0) for s in send]
        got_parts, got_extra = swap_with((parts, extra), axis, bit)
        got = [jnp.concatenate(g, 0) if pieces > 1 else g[0] for g in got_parts]
        blocks = [k + g.astype(jnp.float32) for k, g in zip(keep, got)]
        extra = extra + got_extra
    return [b[0] for b in blocks], extra


def norm_gelu(values):
    centered = values - jnp.mean(values, -1, keepdims=True)
    variance = jnp.mean(centered * centered, -1, keepdims=True)
    return jax.nn.gelu(centered * lax.rsqrt(variance + 1e-05))


def spread(source_field, shard_reach):
    near_pieces = {}
    far_pieces = {}
    for direction in (1, -1):
        near_pieces[direction] = from_behind(source_field, "seq", direction * shard_reach)
    for direction in (1, -1):
        far_pieces[direction] = from_behind(source_field, "seq", 2 * direction * shard_reach)
    return [far_pieces[1], near_pieces[1], source_field, near_pieces[-1], far_pieces[-1]]


def shards(tokens, mask_flags, hidden_in, grad_above, w_in, conv_weight, w_out, head_weight):
    local_rows = tokens.shape[0]
    vocab_size = head_weight.shape[1]
    seq_devices = lax.axis_size("seq")
    shard_reach = 4
    context_rows = float(local_rows * seq_devices)
    masked = mask_flags.astype(jnp.float32)
    local_count = jnp.sum(masked)
    mask_total = count_sum(jnp.broadcast_to(local_count, (8, 128)), "seq")[0, 0]
    alphabet = jnp.arange(vocab_size, dtype=jnp.int32)
    first_act = norm_gelu(hidden_in.astype(jnp.float32)).astype(jnp.bfloat16)
    first_pre = jnp.dot(first_act, w_in, preferred_element_type=jnp.float32)
    narrow_activation = norm_gelu(first_pre).astype(jnp.bfloat16)
    kernel_tap_pile = jnp.stack(spread(narrow_activation, shard_reach))
    conv_pre = jnp.einsum(
        "krc,kcb->rb", kernel_tap_pile, conv_weight, preferred_element_type=jnp.float32
    )
    conv_act = norm_gelu(conv_pre).astype(jnp.bfloat16)
    projected = lax.dot_general(
        conv_act, w_out, (((1,), (1,)), ((), ())), preferred_element_type=jnp.float32
    )
    block_out = (hidden_in.astype(jnp.float32) + projected).astype(jnp.bfloat16)
    logits_t = lax.dot_general(
        head_weight, block_out, (((0,), (1,)), ((), ())), preferred_element_type=jnp.float32
    )
    log_total = jnp.log(jnp.sum(jnp.exp(logits_t), 0))
    target_hot = (alphabet[:, None] == tokens[None, :]).astype(jnp.float32)
    cross_ent = log_total - jnp.sum(target_hot * logits_t, 0)
    local_loss = jnp.sum(masked * cross_ent)
    probability = jnp.exp(logits_t - log_total[None, :])
    grad_logits = (
        masked[None, :] * (probability - target_hot) * (context_rows / mask_total)
    ).astype(jnp.bfloat16)
    head_part = lax.dot_general(
        grad_logits, head_weight, (((0,), (1,)), ((), ())), preferred_element_type=jnp.float32
    )
    grad_block = (head_part + grad_above.astype(jnp.float32)).astype(jnp.bfloat16)
    columns = tree_layout(grad_block, "seq")
    down_partial = lax.dot_general(
        columns, conv_act, (((0,), (0,)), ((), ())), preferred_element_type=jnp.float32
    )
    grad_conv_act = jnp.dot(grad_block, w_out, preferred_element_type=jnp.float32)
    gradient_before_activation = jax.vjp(norm_gelu, conv_pre)[1](grad_conv_act)[0].astype(
        jnp.bfloat16
    )
    back_pieces = spread(gradient_before_activation, shard_reach)
    backward_tap_pile = jnp.stack(back_pieces[::-1])
    grad_neck = jnp.einsum(
        "krc,kbc->rb", backward_tap_pile, conv_weight, preferred_element_type=jnp.float32
    )
    grad_first = jax.vjp(norm_gelu, first_pre)[1](grad_neck)[0].astype(jnp.bfloat16)
    columns = tree_layout(first_act, "seq")
    up_partial = lax.dot_general(
        columns, grad_first, (((0,), (0,)), ((), ())), preferred_element_type=jnp.float32
    )
    (grad_down, grad_up), loss_tile = tree_scatter(
        (down_partial, up_partial), jnp.broadcast_to(local_loss, (8, 128)), "seq"
    )
    grad_down = grad_down.astype(jnp.bfloat16)
    grad_up = grad_up.astype(jnp.bfloat16)
    loss_total = loss_tile[0, 0]
    return (loss_total / mask_total, grad_up, grad_down)


def solution(mesh):
    placed = (P("seq"), P("seq"), P("seq", None), P("seq", None), P(), P(), P(), P())
    return jax.shard_map(
        shards,
        mesh=mesh,
        in_specs=placed,
        out_specs=(P(), P("seq", None), P("seq", None)),
        check_vma=False,
    )
```

```python
import jax
import jax.numpy as jnp
from jax import lax
from jax.sharding import PartitionSpec as P


def from_behind(block, axis, distance):
    devices = range(lax.axis_size(axis))
    route = [(i - distance, i) for i in devices if i - distance in devices]
    return lax.ppermute(block, axis, route)


def swap_with(block, axis, bit):
    devices = lax.axis_size(axis)
    return lax.ppermute(block, axis, [(i, i ^ bit) for i in range(devices)])


def link_order(devices):
    bits = [1 << k for k in range(devices.bit_length() - 1)]
    near = [1, 2, 16, 64, 4, 32, 128, 8]
    return [b for b in near if b in bits] + [b for b in bits if b not in near]


def tree_sum(values, axis):
    for bit in link_order(lax.axis_size(axis)):
        values = values + swap_with(values, axis, bit)
    return values


def count_sum(counts, axis):
    order = link_order(lax.axis_size(axis))
    for first, second in zip(order[0::2], order[1::2]):
        counts = (
            counts
            + swap_with(counts, axis, first)
            + swap_with(counts, axis, second)
            + swap_with(counts, axis, first ^ second)
        )
    return counts


def tree_layout(columns, axis):
    devices = lax.axis_size(axis)
    depth = devices.bit_length() - 1
    rows, width = columns.shape
    split = columns.reshape((rows,) + (2,) * depth + (width // devices,))
    axes = [1 + depth - 1 - (bit.bit_length() - 1) for bit in link_order(devices)]
    return split.transpose([0] + axes + [depth + 1]).reshape(rows, width)


def tree_scatter(partials, extra, axis):
    devices = lax.axis_size(axis)
    me = lax.axis_index(axis)
    blocks = [p.reshape(devices, p.shape[0] // devices, -1) for p in partials]
    for bit in link_order(devices):
        half = blocks[0].shape[0] // 2
        upper = (me // bit) % 2
        keep = [lax.dynamic_slice_in_dim(b, upper * half, half, 0) for b in blocks]
        send = [
            lax.dynamic_slice_in_dim(b, (1 - upper) * half, half, 0).astype(jnp.bfloat16)
            for b in blocks
        ]
        pieces = 4 if half >= 32 else (2 if half >= 16 else 1)
        parts = [jnp.split(s, pieces, 0) for s in send]
        got_parts, got_extra = swap_with((parts, extra), axis, bit)
        got = [jnp.concatenate(g, 0) if pieces > 1 else g[0] for g in got_parts]
        blocks = [k + g.astype(jnp.float32) for k, g in zip(keep, got)]
        extra = extra + got_extra
    return [b[0] for b in blocks], extra


def norm_gelu(values):
    centered = values - jnp.mean(values, -1, keepdims=True)
    variance = jnp.mean(centered * centered, -1, keepdims=True)
    return jax.nn.gelu(centered * lax.rsqrt(variance + 1e-05))


def spread(source_field, shard_reach):
    near_pieces = {}
    far_pieces = {}
    for direction in (1, -1):
        near_pieces[direction] = from_behind(source_field, "seq", direction * shard_reach)
    for direction in (1, -1):
        far_pieces[direction] = from_behind(source_field, "seq", 2 * direction * shard_reach)
    return [far_pieces[1], near_pieces[1], source_field, near_pieces[-1], far_pieces[-1]]


def shards(tokens, mask_flags, hidden_in, grad_above, w_in, conv_weight, w_out, head_weight):
    local_rows = tokens.shape[0]
    vocab_size = head_weight.shape[1]
    seq_devices = lax.axis_size("seq")
    shard_reach = 4
    context_rows = float(local_rows * seq_devices)
    masked = mask_flags.astype(jnp.float32)
    local_count = jnp.sum(masked)
    mask_total = count_sum(jnp.broadcast_to(local_count, (8, 128)), "seq")[0, 0]
    alphabet = jnp.arange(vocab_size, dtype=jnp.int32)
    first_act = norm_gelu(hidden_in.astype(jnp.float32)).astype(jnp.bfloat16)
    first_pre = jnp.dot(first_act, w_in, preferred_element_type=jnp.float32)
    narrow_activation = norm_gelu(first_pre).astype(jnp.bfloat16)
    kernel_tap_pile = jnp.stack(spread(narrow_activation, shard_reach))
    conv_pre = jnp.einsum(
        "krc,kcb->rb", kernel_tap_pile, conv_weight, preferred_element_type=jnp.float32
    )
    conv_act = norm_gelu(conv_pre).astype(jnp.bfloat16)
    projected = lax.dot_general(
        conv_act, w_out, (((1,), (1,)), ((), ())), preferred_element_type=jnp.float32
    )
    block_out = (hidden_in.astype(jnp.float32) + projected).astype(jnp.bfloat16)
    logits_t = lax.dot_general(
        head_weight, block_out, (((0,), (1,)), ((), ())), preferred_element_type=jnp.float32
    )
    log_total = jnp.log(jnp.sum(jnp.exp(logits_t), 0))
    target_hot = (alphabet[:, None] == tokens[None, :]).astype(jnp.float32)
    cross_ent = log_total - jnp.sum(target_hot * logits_t, 0)
    local_loss = jnp.sum(masked * cross_ent)
    probability = jnp.exp(logits_t - log_total[None, :])
    grad_logits = (
        masked[None, :] * (probability - target_hot) * (context_rows / mask_total)
    ).astype(jnp.bfloat16)
    head_part = lax.dot_general(
        grad_logits, head_weight, (((0,), (1,)), ((), ())), preferred_element_type=jnp.float32
    )
    grad_block = (head_part + grad_above.astype(jnp.float32)).astype(jnp.bfloat16)
    columns = tree_layout(grad_block, "seq")
    down_partial = lax.dot_general(
        columns, conv_act, (((0,), (0,)), ((), ())), preferred_element_type=jnp.float32
    )
    grad_conv_act = jnp.dot(grad_block, w_out, preferred_element_type=jnp.float32)
    gradient_before_activation = jax.vjp(norm_gelu, conv_pre)[1](grad_conv_act)[0].astype(
        jnp.bfloat16
    )
    back_pieces = spread(gradient_before_activation, shard_reach)
    backward_tap_pile = jnp.stack(back_pieces[::-1])
    grad_neck = jnp.einsum(
        "krc,kbc->rb", backward_tap_pile, conv_weight, preferred_element_type=jnp.float32
    )
    grad_first = jax.vjp(norm_gelu, first_pre)[1](grad_neck)[0].astype(jnp.bfloat16)
    columns = tree_layout(first_act, "seq")
    up_partial = lax.dot_general(
        columns, grad_first, (((0,), (0,)), ((), ())), preferred_element_type=jnp.float32
    )
    (grad_down, grad_up), loss_tile = tree_scatter(
        (down_partial, up_partial), jnp.broadcast_to(local_loss, (8, 128)), "seq"
    )
    grad_down = grad_down.astype(jnp.bfloat16)
    grad_up = grad_up.astype(jnp.bfloat16)
    loss_total = loss_tile[0, 0]
    return (loss_total / mask_total, grad_up, grad_down)


def solution(mesh):
    placed = (P("seq"), P("seq"), P("seq", None), P("seq", None), P(), P(), P(), P())
    return jax.shard_map(
        shards,
        mesh=mesh,
        in_specs=placed,
        out_specs=(P(), P("seq", None), P("seq", None)),
        check_vma=False,
    )
```

```python
import jax
import jax.numpy as jnp
from jax import lax
from jax.sharding import PartitionSpec as P


def from_behind(block, axis, distance):
    devices = range(lax.axis_size(axis))
    route = [(i - distance, i) for i in devices if i - distance in devices]
    return jnp.concatenate(lax.ppermute(jnp.split(block, 2, 0), axis, route), 0)


def swap_with(block, axis, bit):
    devices = lax.axis_size(axis)
    return lax.ppermute(block, axis, [(i, i ^ bit) for i in range(devices)])


def link_order(devices):
    bits = [1 << k for k in range(devices.bit_length() - 1)]
    near = [1, 2, 16, 64, 4, 32, 128, 8]
    return [b for b in near if b in bits] + [b for b in bits if b not in near]


def tree_sum(values, axis):
    for bit in link_order(lax.axis_size(axis)):
        values = values + swap_with(values, axis, bit)
    return values


def count_sum(counts, axis):
    order = link_order(lax.axis_size(axis))
    for first, second in zip(order[0::2], order[1::2]):
        counts = (
            counts
            + swap_with(counts, axis, first)
            + swap_with(counts, axis, second)
            + swap_with(counts, axis, first ^ second)
        )
    return counts


def tree_layout(columns, axis):
    devices = lax.axis_size(axis)
    depth = devices.bit_length() - 1
    rows, width = columns.shape
    split = columns.reshape((rows,) + (2,) * depth + (width // devices,))
    axes = [1 + depth - 1 - (bit.bit_length() - 1) for bit in link_order(devices)]
    return split.transpose([0] + axes + [depth + 1]).reshape(rows, width)


def tree_scatter(partials, extra, axis):
    devices = lax.axis_size(axis)
    me = lax.axis_index(axis)
    blocks = [p.reshape(devices, p.shape[0] // devices, -1) for p in partials]
    for bit in link_order(devices):
        half = blocks[0].shape[0] // 2
        upper = (me // bit) % 2
        keep = [lax.dynamic_slice_in_dim(b, upper * half, half, 0) for b in blocks]
        send = [
            lax.dynamic_slice_in_dim(b, (1 - upper) * half, half, 0).astype(jnp.bfloat16)
            for b in blocks
        ]
        pieces = 2 if half >= 16 else 1
        parts = [jnp.split(s, pieces, 0) for s in send]
        got_parts, got_extra = swap_with((parts, extra), axis, bit)
        got = [jnp.concatenate(g, 0) if pieces > 1 else g[0] for g in got_parts]
        blocks = [k + g.astype(jnp.float32) for k, g in zip(keep, got)]
        extra = extra + got_extra
    return [b[0] for b in blocks], extra


def norm_gelu(values):
    centered = values - jnp.mean(values, -1, keepdims=True)
    variance = jnp.mean(centered * centered, -1, keepdims=True)
    return jax.nn.gelu(centered * lax.rsqrt(variance + 1e-05))


def spread(source_field, shard_reach):
    near_pieces = {}
    far_pieces = {}
    for direction in (1, -1):
        near_pieces[direction] = from_behind(source_field, "seq", direction * shard_reach)
    for direction in (1, -1):
        far_pieces[direction] = from_behind(source_field, "seq", 2 * direction * shard_reach)
    return [far_pieces[1], near_pieces[1], source_field, near_pieces[-1], far_pieces[-1]]


def shards(tokens, mask_flags, hidden_in, grad_above, w_in, conv_weight, w_out, head_weight):
    local_rows = tokens.shape[0]
    vocab_size = head_weight.shape[1]
    seq_devices = lax.axis_size("seq")
    shard_reach = 4
    context_rows = float(local_rows * seq_devices)
    masked = mask_flags.astype(jnp.float32)
    local_count = jnp.sum(masked)
    mask_total = count_sum(jnp.broadcast_to(local_count, (8, 128)), "seq")[0, 0]
    alphabet = jnp.arange(vocab_size, dtype=jnp.int32)
    first_act = norm_gelu(hidden_in.astype(jnp.float32)).astype(jnp.bfloat16)
    first_pre = jnp.dot(first_act, w_in, preferred_element_type=jnp.float32)
    narrow_activation = norm_gelu(first_pre).astype(jnp.bfloat16)
    kernel_tap_pile = jnp.stack(spread(narrow_activation, shard_reach))
    conv_pre = jnp.einsum(
        "krc,kcb->rb", kernel_tap_pile, conv_weight, preferred_element_type=jnp.float32
    )
    conv_act = norm_gelu(conv_pre).astype(jnp.bfloat16)
    projected = lax.dot_general(
        conv_act, w_out, (((1,), (1,)), ((), ())), preferred_element_type=jnp.float32
    )
    block_out = (hidden_in.astype(jnp.float32) + projected).astype(jnp.bfloat16)
    logits_t = lax.dot_general(
        head_weight, block_out, (((0,), (1,)), ((), ())), preferred_element_type=jnp.float32
    )
    log_total = jnp.log(jnp.sum(jnp.exp(logits_t), 0))
    target_hot = (alphabet[:, None] == tokens[None, :]).astype(jnp.float32)
    cross_ent = log_total - jnp.sum(target_hot * logits_t, 0)
    local_loss = jnp.sum(masked * cross_ent)
    probability = jnp.exp(logits_t - log_total[None, :])
    grad_logits = (
        masked[None, :] * (probability - target_hot) * (context_rows / mask_total)
    ).astype(jnp.bfloat16)
    head_part = lax.dot_general(
        grad_logits, head_weight, (((0,), (1,)), ((), ())), preferred_element_type=jnp.float32
    )
    grad_block = (head_part + grad_above.astype(jnp.float32)).astype(jnp.bfloat16)
    columns = tree_layout(grad_block, "seq")
    down_partial = lax.dot_general(
        columns, conv_act, (((0,), (0,)), ((), ())), preferred_element_type=jnp.float32
    )
    grad_conv_act = jnp.dot(grad_block, w_out, preferred_element_type=jnp.float32)
    gradient_before_activation = jax.vjp(norm_gelu, conv_pre)[1](grad_conv_act)[0].astype(
        jnp.bfloat16
    )
    back_pieces = spread(gradient_before_activation, shard_reach)
    backward_tap_pile = jnp.stack(back_pieces[::-1])
    grad_neck = jnp.einsum(
        "krc,kbc->rb", backward_tap_pile, conv_weight, preferred_element_type=jnp.float32
    )
    grad_first = jax.vjp(norm_gelu, first_pre)[1](grad_neck)[0].astype(jnp.bfloat16)
    columns = tree_layout(first_act, "seq")
    up_partial = lax.dot_general(
        columns, grad_first, (((0,), (0,)), ((), ())), preferred_element_type=jnp.float32
    )
    (grad_down, grad_up), loss_tile = tree_scatter(
        (down_partial, up_partial), jnp.broadcast_to(local_loss, (8, 128)), "seq"
    )
    grad_down = grad_down.astype(jnp.bfloat16)
    grad_up = grad_up.astype(jnp.bfloat16)
    loss_total = loss_tile[0, 0]
    return (loss_total / mask_total, grad_up, grad_down)


def solution(mesh):
    placed = (P("seq"), P("seq"), P("seq", None), P("seq", None), P(), P(), P(), P())
    return jax.shard_map(
        shards,
        mesh=mesh,
        in_specs=placed,
        out_specs=(P(), P("seq", None), P("seq", None)),
        check_vma=False,
    )
```

```python
import jax
import jax.numpy as jnp
from jax import lax
from jax.sharding import PartitionSpec as P


def from_behind(block, axis, distance):
    devices = range(lax.axis_size(axis))
    route = [(i - distance, i) for i in devices if i - distance in devices]
    return lax.ppermute(block, axis, route)


def swap_with(block, axis, bit):
    devices = lax.axis_size(axis)
    return lax.ppermute(block, axis, [(i, i ^ bit) for i in range(devices)])


def link_order(devices):
    bits = [1 << k for k in range(devices.bit_length() - 1)]
    near = [1, 2, 16, 64, 4, 32, 128, 8]
    return [b for b in near if b in bits] + [b for b in bits if b not in near]


def tree_sum(values, axis):
    for bit in link_order(lax.axis_size(axis)):
        values = values + swap_with(values, axis, bit)
    return values


def count_sum(counts, axis):
    order = link_order(lax.axis_size(axis))
    for first, second in zip(order[0::2], order[1::2]):
        counts = (
            counts
            + swap_with(counts, axis, first)
            + swap_with(counts, axis, second)
            + swap_with(counts, axis, first ^ second)
        )
    return counts


def tree_layout(columns, axis):
    devices = lax.axis_size(axis)
    depth = devices.bit_length() - 1
    rows, width = columns.shape
    split = columns.reshape((rows,) + (2,) * depth + (width // devices,))
    axes = [1 + depth - 1 - (bit.bit_length() - 1) for bit in link_order(devices)]
    return split.transpose([0] + axes + [depth + 1]).reshape(rows, width)


def split_pair(value):
    high = value.astype(jnp.bfloat16)
    low = (value - high.astype(jnp.float32)).astype(jnp.bfloat16)
    return high, low


def tree_scatter(partials, extra, axis):
    devices = lax.axis_size(axis)
    me = lax.axis_index(axis)
    blocks = [p.reshape(devices, p.shape[0] // devices, -1) for p in partials]
    share, width = blocks[0].shape[1:]
    for bit in link_order(devices):
        half = blocks[0].shape[0] // 2
        upper = (me // bit) % 2
        keep = [lax.dynamic_slice_in_dim(b, upper * half, half, 0) for b in blocks]
        send = [
            lax.dynamic_slice_in_dim(b, (1 - upper) * half, half, 0).astype(jnp.bfloat16)
            for b in blocks
        ]
        pieces = 2 if half >= 16 else 1
        parts = [list(jnp.split(s, pieces, 0)) for s in send]
        high, low = split_pair(extra)
        extra = high.astype(jnp.float32) + low.astype(jnp.float32)
        rows = parts[0][0].shape[0]
        tail = jnp.concatenate(
            [jnp.broadcast_to(high, (rows, 1, width // 2)), jnp.broadcast_to(low, (rows, 1, width // 2))],
            2,
        )
        parts[0][0] = jnp.concatenate([parts[0][0], tail], 1)
        got_parts = swap_with(parts, axis, bit)
        got_tail = got_parts[0][0][0, share].astype(jnp.float32)
        extra = extra + (got_tail[0] + got_tail[width // 2])
        got_parts[0][0] = got_parts[0][0][:, :share]
        got = [jnp.concatenate(g, 0) if pieces > 1 else g[0] for g in got_parts]
        blocks = [k + g.astype(jnp.float32) for k, g in zip(keep, got)]
    return [b[0] for b in blocks], extra


def norm_gelu(values):
    centered = values - jnp.mean(values, -1, keepdims=True)
    variance = jnp.mean(centered * centered, -1, keepdims=True)
    return jax.nn.gelu(centered * lax.rsqrt(variance + 1e-05))


def spread(source_field, shard_reach):
    near_pieces = {}
    far_pieces = {}
    for direction in (1, -1):
        near_pieces[direction] = from_behind(source_field, "seq", direction * shard_reach)
    for direction in (1, -1):
        far_pieces[direction] = from_behind(source_field, "seq", 2 * direction * shard_reach)
    return [far_pieces[1], near_pieces[1], source_field, near_pieces[-1], far_pieces[-1]]


def shards(tokens, mask_flags, hidden_in, grad_above, w_in, conv_weight, w_out, head_weight):
    local_rows = tokens.shape[0]
    vocab_size = head_weight.shape[1]
    seq_devices = lax.axis_size("seq")
    shard_reach = 4
    context_rows = float(local_rows * seq_devices)
    masked = mask_flags.astype(jnp.float32)
    local_count = jnp.sum(masked)
    mask_total = count_sum(jnp.broadcast_to(local_count, (8, 128)), "seq")[0, 0]
    alphabet = jnp.arange(vocab_size, dtype=jnp.int32)
    first_act = norm_gelu(hidden_in.astype(jnp.float32)).astype(jnp.bfloat16)
    first_pre = jnp.dot(first_act, w_in, preferred_element_type=jnp.float32)
    narrow_activation = norm_gelu(first_pre).astype(jnp.bfloat16)
    kernel_tap_pile = jnp.stack(spread(narrow_activation, shard_reach))
    conv_pre = jnp.einsum(
        "krc,kcb->rb", kernel_tap_pile, conv_weight, preferred_element_type=jnp.float32
    )
    conv_act = norm_gelu(conv_pre).astype(jnp.bfloat16)
    projected = lax.dot_general(
        conv_act, w_out, (((1,), (1,)), ((), ())), preferred_element_type=jnp.float32
    )
    block_out = (hidden_in.astype(jnp.float32) + projected).astype(jnp.bfloat16)
    logits_t = lax.dot_general(
        head_weight, block_out, (((0,), (1,)), ((), ())), preferred_element_type=jnp.float32
    )
    log_total = jnp.log(jnp.sum(jnp.exp(logits_t), 0))
    target_hot = (alphabet[:, None] == tokens[None, :]).astype(jnp.float32)
    cross_ent = log_total - jnp.sum(target_hot * logits_t, 0)
    local_loss = jnp.sum(masked * cross_ent)
    probability = jnp.exp(logits_t - log_total[None, :])
    grad_logits = (
        masked[None, :] * (probability - target_hot) * (context_rows / mask_total)
    ).astype(jnp.bfloat16)
    head_part = lax.dot_general(
        grad_logits, head_weight, (((0,), (1,)), ((), ())), preferred_element_type=jnp.float32
    )
    grad_block = (head_part + grad_above.astype(jnp.float32)).astype(jnp.bfloat16)
    columns = tree_layout(grad_block, "seq")
    down_partial = lax.dot_general(
        columns, conv_act, (((0,), (0,)), ((), ())), preferred_element_type=jnp.float32
    )
    grad_conv_act = jnp.dot(grad_block, w_out, preferred_element_type=jnp.float32)
    gradient_before_activation = jax.vjp(norm_gelu, conv_pre)[1](grad_conv_act)[0].astype(
        jnp.bfloat16
    )
    back_pieces = spread(gradient_before_activation, shard_reach)
    backward_tap_pile = jnp.stack(back_pieces[::-1])
    grad_neck = jnp.einsum(
        "krc,kbc->rb", backward_tap_pile, conv_weight, preferred_element_type=jnp.float32
    )
    grad_first = jax.vjp(norm_gelu, first_pre)[1](grad_neck)[0].astype(jnp.bfloat16)
    columns = tree_layout(first_act, "seq")
    up_partial = lax.dot_general(
        columns, grad_first, (((0,), (0,)), ((), ())), preferred_element_type=jnp.float32
    )
    (grad_down, grad_up), loss_total = tree_scatter((down_partial, up_partial), local_loss, "seq")
    grad_down = grad_down.astype(jnp.bfloat16)
    grad_up = grad_up.astype(jnp.bfloat16)
    return (loss_total / mask_total, grad_up, grad_down)


def solution(mesh):
    placed = (P("seq"), P("seq"), P("seq", None), P("seq", None), P(), P(), P(), P())
    return jax.shard_map(
        shards,
        mesh=mesh,
        in_specs=placed,
        out_specs=(P(), P("seq", None), P("seq", None)),
        check_vma=False,
    )
```

```python
import jax
import jax.numpy as jnp
from jax import lax
from jax.sharding import PartitionSpec as P


def from_behind(block, axis, distance):
    devices = range(lax.axis_size(axis))
    route = [(i - distance, i) for i in devices if i - distance in devices]
    return lax.ppermute(block, axis, route)


def swap_with(block, axis, bit):
    devices = lax.axis_size(axis)
    return lax.ppermute(block, axis, [(i, i ^ bit) for i in range(devices)])


def link_order(devices):
    bits = [1 << k for k in range(devices.bit_length() - 1)]
    near = [1, 2, 16, 64, 4, 32, 128, 8]
    return [b for b in near if b in bits] + [b for b in bits if b not in near]


def tree_sum(values, axis):
    for bit in link_order(lax.axis_size(axis)):
        values = values + swap_with(values, axis, bit)
    return values


def count_sum(counts, axis):
    order = link_order(lax.axis_size(axis))
    for first, second in zip(order[0::2], order[1::2]):
        counts = (
            counts
            + swap_with(counts, axis, first)
            + swap_with(counts, axis, second)
            + swap_with(counts, axis, first ^ second)
        )
    return counts


def tree_layout(columns, axis):
    devices = lax.axis_size(axis)
    depth = devices.bit_length() - 1
    rows, width = columns.shape
    split = columns.reshape((rows,) + (2,) * depth + (width // devices,))
    axes = [1 + depth - 1 - (bit.bit_length() - 1) for bit in link_order(devices)]
    return split.transpose([0] + axes + [depth + 1]).reshape(rows, width)


def tree_scatter(partials, extra, axis):
    devices = lax.axis_size(axis)
    me = lax.axis_index(axis)
    blocks = [p.reshape(devices, p.shape[0] // devices, -1) for p in partials]
    for bit in link_order(devices):
        half = blocks[0].shape[0] // 2
        upper = (me // bit) % 2
        keep = [lax.dynamic_slice_in_dim(b, upper * half, half, 0) for b in blocks]
        send = [
            lax.dynamic_slice_in_dim(b, (1 - upper) * half, half, 0).astype(jnp.bfloat16)
            for b in blocks
        ]
        pieces = 2 if half >= 16 else 1
        parts = [jnp.split(s, pieces, 0) for s in send]
        got_parts, got_extra = swap_with((parts, extra), axis, bit)
        got = [jnp.concatenate(g, 0) if pieces > 1 else g[0] for g in got_parts]
        blocks = [k + g.astype(jnp.float32) for k, g in zip(keep, got)]
        extra = extra + got_extra
    return [b[0] for b in blocks], extra


def norm_gelu(values):
    centered = values - jnp.mean(values, -1, keepdims=True)
    variance = jnp.mean(centered * centered, -1, keepdims=True)
    return jax.nn.gelu(centered * lax.rsqrt(variance + 1e-05))


def spread(source_field, shard_reach):
    near_pieces = {}
    far_pieces = {}
    for direction in (1, -1):
        near_pieces[direction] = from_behind(source_field, "seq", direction * shard_reach)
    for direction in (1, -1):
        far_pieces[direction] = from_behind(source_field, "seq", 2 * direction * shard_reach)
    return [far_pieces[1], near_pieces[1], source_field, near_pieces[-1], far_pieces[-1]]


def shards(tokens, mask_flags, hidden_in, grad_above, w_in, conv_weight, w_out, head_weight):
    local_rows = tokens.shape[0]
    vocab_size = head_weight.shape[1]
    seq_devices = lax.axis_size("seq")
    shard_reach = 4
    context_rows = float(local_rows * seq_devices)
    masked = mask_flags.astype(jnp.float32)
    local_count = jnp.sum(masked)
    count_tile = count_sum(jnp.broadcast_to(local_count, (8, 128)), "seq")
    alphabet = jnp.arange(vocab_size, dtype=jnp.int32)
    first_act = norm_gelu(hidden_in.astype(jnp.float32)).astype(jnp.bfloat16)
    first_pre = jnp.dot(first_act, w_in, preferred_element_type=jnp.float32)
    narrow_activation = norm_gelu(first_pre).astype(jnp.bfloat16)
    count_tile, narrow_activation = lax.optimization_barrier((count_tile, narrow_activation))
    mask_total = count_tile[0, 0]
    kernel_tap_pile = jnp.stack(spread(narrow_activation, shard_reach))
    conv_pre = jnp.einsum(
        "krc,kcb->rb", kernel_tap_pile, conv_weight, preferred_element_type=jnp.float32
    )
    conv_act = norm_gelu(conv_pre).astype(jnp.bfloat16)
    projected = lax.dot_general(
        conv_act, w_out, (((1,), (1,)), ((), ())), preferred_element_type=jnp.float32
    )
    block_out = (hidden_in.astype(jnp.float32) + projected).astype(jnp.bfloat16)
    logits_t = lax.dot_general(
        head_weight, block_out, (((0,), (1,)), ((), ())), preferred_element_type=jnp.float32
    )
    log_total = jnp.log(jnp.sum(jnp.exp(logits_t), 0))
    target_hot = (alphabet[:, None] == tokens[None, :]).astype(jnp.float32)
    cross_ent = log_total - jnp.sum(target_hot * logits_t, 0)
    local_loss = jnp.sum(masked * cross_ent)
    probability = jnp.exp(logits_t - log_total[None, :])
    grad_logits = (
        masked[None, :] * (probability - target_hot) * (context_rows / mask_total)
    ).astype(jnp.bfloat16)
    head_part = lax.dot_general(
        grad_logits, head_weight, (((0,), (1,)), ((), ())), preferred_element_type=jnp.float32
    )
    grad_block = (head_part + grad_above.astype(jnp.float32)).astype(jnp.bfloat16)
    columns = tree_layout(grad_block, "seq")
    down_partial = lax.dot_general(
        columns, conv_act, (((0,), (0,)), ((), ())), preferred_element_type=jnp.float32
    )
    grad_conv_act = jnp.dot(grad_block, w_out, preferred_element_type=jnp.float32)
    gradient_before_activation = jax.vjp(norm_gelu, conv_pre)[1](grad_conv_act)[0].astype(
        jnp.bfloat16
    )
    back_pieces = spread(gradient_before_activation, shard_reach)
    backward_tap_pile = jnp.stack(back_pieces[::-1])
    grad_neck = jnp.einsum(
        "krc,kbc->rb", backward_tap_pile, conv_weight, preferred_element_type=jnp.float32
    )
    grad_first = jax.vjp(norm_gelu, first_pre)[1](grad_neck)[0].astype(jnp.bfloat16)
    columns = tree_layout(first_act, "seq")
    up_partial = lax.dot_general(
        columns, grad_first, (((0,), (0,)), ((), ())), preferred_element_type=jnp.float32
    )
    (grad_down, grad_up), loss_tile = tree_scatter(
        (down_partial, up_partial), jnp.broadcast_to(local_loss, (8, 128)), "seq"
    )
    grad_down = grad_down.astype(jnp.bfloat16)
    grad_up = grad_up.astype(jnp.bfloat16)
    loss_total = loss_tile[0, 0]
    return (loss_total / mask_total, grad_up, grad_down)


def solution(mesh):
    placed = (P("seq"), P("seq"), P("seq", None), P("seq", None), P(), P(), P(), P())
    return jax.shard_map(
        shards,
        mesh=mesh,
        in_specs=placed,
        out_specs=(P(), P("seq", None), P("seq", None)),
        check_vma=False,
    )
```

```python
import jax
import jax.numpy as jnp
from jax import lax
from jax.sharding import PartitionSpec as P


def from_behind(block, axis, distance):
    devices = range(lax.axis_size(axis))
    route = [(i - distance, i) for i in devices if i - distance in devices]
    return lax.ppermute(block, axis, route)


def swap_with(block, axis, bit):
    devices = lax.axis_size(axis)
    return lax.ppermute(block, axis, [(i, i ^ bit) for i in range(devices)])


def link_order(devices):
    bits = [1 << k for k in range(devices.bit_length() - 1)]
    near = [1, 2, 16, 64, 4, 32, 128, 8]
    return [b for b in near if b in bits] + [b for b in bits if b not in near]


def tree_sum(values, axis):
    for bit in link_order(lax.axis_size(axis)):
        values = values + swap_with(values, axis, bit)
    return values


def count_sum(counts, axis):
    order = link_order(lax.axis_size(axis))
    for first, second in zip(order[0::2], order[1::2]):
        counts = (
            counts
            + swap_with(counts, axis, first)
            + swap_with(counts, axis, second)
            + swap_with(counts, axis, first ^ second)
        )
    return counts


def tree_layout(columns, axis):
    devices = lax.axis_size(axis)
    depth = devices.bit_length() - 1
    rows, width = columns.shape
    split = columns.reshape((rows,) + (2,) * depth + (width // devices,))
    axes = [1 + depth - 1 - (bit.bit_length() - 1) for bit in link_order(devices)]
    return split.transpose([0] + axes + [depth + 1]).reshape(rows, width)


def tree_scatter(partials, extra, axis):
    devices = lax.axis_size(axis)
    me = lax.axis_index(axis)
    blocks = [p.reshape(devices, p.shape[0] // devices, -1) for p in partials]
    for bit in link_order(devices):
        half = blocks[0].shape[0] // 2
        upper = (me // bit) % 2
        keep = [lax.dynamic_slice_in_dim(b, upper * half, half, 0) for b in blocks]
        send = [
            lax.dynamic_slice_in_dim(b, (1 - upper) * half, half, 0).astype(jnp.bfloat16)
            for b in blocks
        ]
        pieces = 2 if half >= 16 else 1
        parts = [jnp.split(s, pieces, 0) for s in send]
        got_parts, got_extra = swap_with((parts, extra), axis, bit)
        got = [jnp.concatenate(g, 0) if pieces > 1 else g[0] for g in got_parts]
        blocks = [k + g.astype(jnp.float32) for k, g in zip(keep, got)]
        if extra is not None:
            extra = extra + got_extra
    return [b[0] for b in blocks], extra


def norm_gelu(values):
    centered = values - jnp.mean(values, -1, keepdims=True)
    variance = jnp.mean(centered * centered, -1, keepdims=True)
    return jax.nn.gelu(centered * lax.rsqrt(variance + 1e-05))


def spread(source_field, shard_reach):
    near_pieces = {}
    far_pieces = {}
    for direction in (1, -1):
        near_pieces[direction] = from_behind(source_field, "seq", direction * shard_reach)
    for direction in (1, -1):
        far_pieces[direction] = from_behind(source_field, "seq", 2 * direction * shard_reach)
    return [far_pieces[1], near_pieces[1], source_field, near_pieces[-1], far_pieces[-1]]


def shards(tokens, mask_flags, hidden_in, grad_above, w_in, conv_weight, w_out, head_weight):
    local_rows = tokens.shape[0]
    vocab_size = head_weight.shape[1]
    seq_devices = lax.axis_size("seq")
    shard_reach = 4
    context_rows = float(local_rows * seq_devices)
    masked = mask_flags.astype(jnp.float32)
    local_count = jnp.sum(masked)
    count_tile = count_sum(jnp.broadcast_to(local_count, (8, 128)), "seq")
    alphabet = jnp.arange(vocab_size, dtype=jnp.int32)
    first_act = norm_gelu(hidden_in.astype(jnp.float32)).astype(jnp.bfloat16)
    first_pre = jnp.dot(first_act, w_in, preferred_element_type=jnp.float32)
    narrow_activation = norm_gelu(first_pre).astype(jnp.bfloat16)
    count_tile, narrow_activation = lax.optimization_barrier((count_tile, narrow_activation))
    mask_total = count_tile[0, 0]
    kernel_tap_pile = jnp.stack(spread(narrow_activation, shard_reach))
    conv_pre = jnp.einsum(
        "krc,kcb->rb", kernel_tap_pile, conv_weight, preferred_element_type=jnp.float32
    )
    conv_act = norm_gelu(conv_pre).astype(jnp.bfloat16)
    projected = lax.dot_general(
        conv_act, w_out, (((1,), (1,)), ((), ())), preferred_element_type=jnp.float32
    )
    block_out = (hidden_in.astype(jnp.float32) + projected).astype(jnp.bfloat16)
    logits_t = lax.dot_general(
        head_weight, block_out, (((0,), (1,)), ((), ())), preferred_element_type=jnp.float32
    )
    log_total = jnp.log(jnp.sum(jnp.exp(logits_t), 0))
    target_hot = (alphabet[:, None] == tokens[None, :]).astype(jnp.float32)
    cross_ent = log_total - jnp.sum(target_hot * logits_t, 0)
    local_loss = jnp.sum(masked * cross_ent)
    probability = jnp.exp(logits_t - log_total[None, :])
    grad_logits = (
        masked[None, :] * (probability - target_hot) * (context_rows / mask_total)
    ).astype(jnp.bfloat16)
    head_part = lax.dot_general(
        grad_logits, head_weight, (((0,), (1,)), ((), ())), preferred_element_type=jnp.float32
    )
    grad_block = (head_part + grad_above.astype(jnp.float32)).astype(jnp.bfloat16)
    columns = tree_layout(grad_block, "seq")
    down_partial = lax.dot_general(
        columns, conv_act, (((0,), (0,)), ((), ())), preferred_element_type=jnp.float32
    )
    grad_conv_act = jnp.dot(grad_block, w_out, preferred_element_type=jnp.float32)
    gradient_before_activation = jax.vjp(norm_gelu, conv_pre)[1](grad_conv_act)[0].astype(
        jnp.bfloat16
    )
    back_pieces = spread(gradient_before_activation, shard_reach)
    backward_tap_pile = jnp.stack(back_pieces[::-1])
    (grad_down,), loss_tile = tree_scatter(
        (down_partial,), jnp.broadcast_to(local_loss, (8, 128)), "seq"
    )
    grad_down, loss_tile, backward_tap_pile = lax.optimization_barrier(
        (grad_down, loss_tile, backward_tap_pile)
    )
    grad_neck = jnp.einsum(
        "krc,kbc->rb", backward_tap_pile, conv_weight, preferred_element_type=jnp.float32
    )
    grad_first = jax.vjp(norm_gelu, first_pre)[1](grad_neck)[0].astype(jnp.bfloat16)
    columns = tree_layout(first_act, "seq")
    up_partial = lax.dot_general(
        columns, grad_first, (((0,), (0,)), ((), ())), preferred_element_type=jnp.float32
    )
    (grad_up,), _ = tree_scatter((up_partial,), None, "seq")
    grad_down = grad_down.astype(jnp.bfloat16)
    grad_up = grad_up.astype(jnp.bfloat16)
    loss_total = loss_tile[0, 0]
    return (loss_total / mask_total, grad_up, grad_down)


def solution(mesh):
    placed = (P("seq"), P("seq"), P("seq", None), P("seq", None), P(), P(), P(), P())
    return jax.shard_map(
        shards,
        mesh=mesh,
        in_specs=placed,
        out_specs=(P(), P("seq", None), P("seq", None)),
        check_vma=False,
    )
```

```python
import jax
import jax.numpy as jnp
from jax import lax
from jax.sharding import PartitionSpec as P


def from_behind(block, axis, distance):
    devices = range(lax.axis_size(axis))
    route = [(i - distance, i) for i in devices if i - distance in devices]
    return lax.ppermute(block, axis, route)


def swap_with(block, axis, bit):
    devices = lax.axis_size(axis)
    return lax.ppermute(block, axis, [(i, i ^ bit) for i in range(devices)])


def link_order(devices):
    bits = [1 << k for k in range(devices.bit_length() - 1)]
    near = [1, 2, 16, 64, 4, 32, 128, 8]
    return [b for b in near if b in bits] + [b for b in bits if b not in near]


def tree_sum(values, axis):
    for bit in link_order(lax.axis_size(axis)):
        values = values + swap_with(values, axis, bit)
    return values


def count_sum(counts, axis):
    order = link_order(lax.axis_size(axis))
    for first, second in zip(order[0::2], order[1::2]):
        counts = (
            counts
            + swap_with(counts, axis, first)
            + swap_with(counts, axis, second)
            + swap_with(counts, axis, first ^ second)
        )
    return counts


def tree_layout(columns, axis):
    devices = lax.axis_size(axis)
    depth = devices.bit_length() - 1
    rows, width = columns.shape
    split = columns.reshape((rows,) + (2,) * depth + (width // devices,))
    axes = [1 + depth - 1 - (bit.bit_length() - 1) for bit in link_order(devices)]
    return split.transpose([0] + axes + [depth + 1]).reshape(rows, width)


def tree_scatter(partials, extra, axis):
    devices = lax.axis_size(axis)
    me = lax.axis_index(axis)
    blocks = [p.reshape(devices, p.shape[0] // devices, -1) for p in partials]
    for bit in link_order(devices):
        half = blocks[0].shape[0] // 2
        upper = (me // bit) % 2
        keep = [lax.dynamic_slice_in_dim(b, upper * half, half, 0) for b in blocks]
        send = [
            lax.dynamic_slice_in_dim(b, (1 - upper) * half, half, 0).astype(jnp.bfloat16)
            for b in blocks
        ]
        pieces = 2 if half >= 16 else 1
        parts = [jnp.split(s, pieces, 0) for s in send]
        got_parts, got_extra = swap_with((parts, extra), axis, bit)
        got = [jnp.concatenate(g, 0) if pieces > 1 else g[0] for g in got_parts]
        blocks = [k + g.astype(jnp.float32) for k, g in zip(keep, got)]
        extra = extra + got_extra
    return [b[0] for b in blocks], extra


def norm_gelu(values):
    centered = values - jnp.mean(values, -1, keepdims=True)
    variance = jnp.mean(centered * centered, -1, keepdims=True)
    return jax.nn.gelu(centered * lax.rsqrt(variance + 1e-05))


def spread(source_field, shard_reach):
    near_pieces = {}
    far_pieces = {}
    for direction in (1, -1):
        near_pieces[direction] = from_behind(source_field, "seq", direction * shard_reach)
    for direction in (1, -1):
        far_pieces[direction] = from_behind(source_field, "seq", 2 * direction * shard_reach)
    return [far_pieces[1], near_pieces[1], source_field, near_pieces[-1], far_pieces[-1]]


def shards(tokens, mask_flags, hidden_in, grad_above, w_in, conv_weight, w_out, head_weight):
    local_rows = tokens.shape[0]
    vocab_size = head_weight.shape[1]
    seq_devices = lax.axis_size("seq")
    shard_reach = 4
    context_rows = float(local_rows * seq_devices)
    masked = mask_flags.astype(jnp.float32)
    local_count = jnp.sum(masked)
    count_tile = count_sum(jnp.broadcast_to(local_count, (8, 128)), "seq")
    alphabet = jnp.arange(vocab_size, dtype=jnp.int32)
    first_act = norm_gelu(hidden_in.astype(jnp.float32)).astype(jnp.bfloat16)
    first_pre = jnp.dot(first_act, w_in, preferred_element_type=jnp.float32)
    narrow_activation = norm_gelu(first_pre).astype(jnp.bfloat16)
    kernel_tap_pile = jnp.stack(spread(narrow_activation, shard_reach))
    count_tile, kernel_tap_pile = lax.optimization_barrier((count_tile, kernel_tap_pile))
    mask_total = count_tile[0, 0]
    conv_pre = jnp.einsum(
        "krc,kcb->rb", kernel_tap_pile, conv_weight, preferred_element_type=jnp.float32
    )
    conv_act = norm_gelu(conv_pre).astype(jnp.bfloat16)
    projected = lax.dot_general(
        conv_act, w_out, (((1,), (1,)), ((), ())), preferred_element_type=jnp.float32
    )
    block_out = (hidden_in.astype(jnp.float32) + projected).astype(jnp.bfloat16)
    logits_t = lax.dot_general(
        head_weight, block_out, (((0,), (1,)), ((), ())), preferred_element_type=jnp.float32
    )
    log_total = jnp.log(jnp.sum(jnp.exp(logits_t), 0))
    target_hot = (alphabet[:, None] == tokens[None, :]).astype(jnp.float32)
    cross_ent = log_total - jnp.sum(target_hot * logits_t, 0)
    local_loss = jnp.sum(masked * cross_ent)
    probability = jnp.exp(logits_t - log_total[None, :])
    grad_logits = (
        masked[None, :] * (probability - target_hot) * (context_rows / mask_total)
    ).astype(jnp.bfloat16)
    head_part = lax.dot_general(
        grad_logits, head_weight, (((0,), (1,)), ((), ())), preferred_element_type=jnp.float32
    )
    grad_block = (head_part + grad_above.astype(jnp.float32)).astype(jnp.bfloat16)
    columns = tree_layout(grad_block, "seq")
    down_partial = lax.dot_general(
        columns, conv_act, (((0,), (0,)), ((), ())), preferred_element_type=jnp.float32
    )
    grad_conv_act = jnp.dot(grad_block, w_out, preferred_element_type=jnp.float32)
    gradient_before_activation = jax.vjp(norm_gelu, conv_pre)[1](grad_conv_act)[0].astype(
        jnp.bfloat16
    )
    back_pieces = spread(gradient_before_activation, shard_reach)
    backward_tap_pile = jnp.stack(back_pieces[::-1])
    grad_neck = jnp.einsum(
        "krc,kbc->rb", backward_tap_pile, conv_weight, preferred_element_type=jnp.float32
    )
    grad_first = jax.vjp(norm_gelu, first_pre)[1](grad_neck)[0].astype(jnp.bfloat16)
    columns = tree_layout(first_act, "seq")
    up_partial = lax.dot_general(
        columns, grad_first, (((0,), (0,)), ((), ())), preferred_element_type=jnp.float32
    )
    (grad_down, grad_up), loss_tile = tree_scatter(
        (down_partial, up_partial), jnp.broadcast_to(local_loss, (8, 128)), "seq"
    )
    grad_down = grad_down.astype(jnp.bfloat16)
    grad_up = grad_up.astype(jnp.bfloat16)
    loss_total = loss_tile[0, 0]
    return (loss_total / mask_total, grad_up, grad_down)


def solution(mesh):
    placed = (P("seq"), P("seq"), P("seq", None), P("seq", None), P(), P(), P(), P())
    return jax.shard_map(
        shards,
        mesh=mesh,
        in_specs=placed,
        out_specs=(P(), P("seq", None), P("seq", None)),
        check_vma=False,
    )
```

```python
import jax
import jax.numpy as jnp
from jax import lax
from jax.sharding import PartitionSpec as P


def from_behind(block, axis, distance):
    devices = range(lax.axis_size(axis))
    route = [(i - distance, i) for i in devices if i - distance in devices]
    return lax.ppermute(block, axis, route)


def swap_with(block, axis, bit):
    devices = lax.axis_size(axis)
    return lax.ppermute(block, axis, [(i, i ^ bit) for i in range(devices)])


def link_order(devices):
    bits = [1 << k for k in range(devices.bit_length() - 1)]
    near = [1, 2, 16, 64, 4, 32, 128, 8]
    return [b for b in near if b in bits] + [b for b in bits if b not in near]


def tree_sum(values, axis):
    for bit in link_order(lax.axis_size(axis)):
        values = values + swap_with(values, axis, bit)
    return values


def count_sum(counts, axis):
    order = link_order(lax.axis_size(axis))
    for first, second in zip(order[0::2], order[1::2]):
        counts = (
            counts
            + swap_with(counts, axis, first)
            + swap_with(counts, axis, second)
            + swap_with(counts, axis, first ^ second)
        )
    return counts


def tree_layout(columns, axis):
    devices = lax.axis_size(axis)
    depth = devices.bit_length() - 1
    rows, width = columns.shape
    split = columns.reshape((rows,) + (2,) * depth + (width // devices,))
    axes = [1 + depth - 1 - (bit.bit_length() - 1) for bit in link_order(devices)]
    return split.transpose([0] + axes + [depth + 1]).reshape(rows, width)


def tree_scatter(partials, extra, axis):
    devices = lax.axis_size(axis)
    me = lax.axis_index(axis)
    blocks = [p.reshape(devices, p.shape[0] // devices, -1) for p in partials]
    for bit in link_order(devices):
        half = blocks[0].shape[0] // 2
        upper = (me // bit) % 2
        keep = [lax.dynamic_slice_in_dim(b, upper * half, half, 0) for b in blocks]
        send = [
            lax.dynamic_slice_in_dim(b, (1 - upper) * half, half, 0).astype(jnp.bfloat16)
            for b in blocks
        ]
        pieces = 2 if half >= 16 else 1
        parts = [jnp.split(s, pieces, 0) for s in send]
        got_parts, got_extra = swap_with((parts, extra), axis, bit)
        got = [jnp.concatenate(g, 0) if pieces > 1 else g[0] for g in got_parts]
        blocks = [k + g.astype(jnp.float32) for k, g in zip(keep, got)]
        extra = extra + got_extra
    return [b[0] for b in blocks], extra


def norm_gelu(values):
    centered = values - jnp.mean(values, -1, keepdims=True)
    variance = jnp.mean(centered * centered, -1, keepdims=True)
    return jax.nn.gelu(centered * lax.rsqrt(variance + 1e-05))


def spread(source_field, shard_reach):
    near_pieces = {}
    far_pieces = {}
    for direction in (1, -1):
        near_pieces[direction] = from_behind(source_field, "seq", direction * shard_reach)
    for direction in (1, -1):
        far_pieces[direction] = from_behind(source_field, "seq", 2 * direction * shard_reach)
    return [far_pieces[1], near_pieces[1], source_field, near_pieces[-1], far_pieces[-1]]


def shards(tokens, mask_flags, hidden_in, grad_above, w_in, conv_weight, w_out, head_weight):
    local_rows = tokens.shape[0]
    vocab_size = head_weight.shape[1]
    seq_devices = lax.axis_size("seq")
    shard_reach = 4
    context_rows = float(local_rows * seq_devices)
    masked = mask_flags.astype(jnp.float32)
    local_count = jnp.sum(masked)
    count_tile = tree_sum(jnp.broadcast_to(local_count, (8, 128)), "seq")
    alphabet = jnp.arange(vocab_size, dtype=jnp.int32)
    first_act = norm_gelu(hidden_in.astype(jnp.float32)).astype(jnp.bfloat16)
    first_pre = jnp.dot(first_act, w_in, preferred_element_type=jnp.float32)
    narrow_activation = norm_gelu(first_pre).astype(jnp.bfloat16)
    kernel_tap_pile = jnp.stack(spread(narrow_activation, shard_reach))
    count_tile, kernel_tap_pile = lax.optimization_barrier((count_tile, kernel_tap_pile))
    mask_total = count_tile[0, 0]
    conv_pre = jnp.einsum(
        "krc,kcb->rb", kernel_tap_pile, conv_weight, preferred_element_type=jnp.float32
    )
    conv_act = norm_gelu(conv_pre).astype(jnp.bfloat16)
    projected = lax.dot_general(
        conv_act, w_out, (((1,), (1,)), ((), ())), preferred_element_type=jnp.float32
    )
    block_out = (hidden_in.astype(jnp.float32) + projected).astype(jnp.bfloat16)
    logits_t = lax.dot_general(
        head_weight, block_out, (((0,), (1,)), ((), ())), preferred_element_type=jnp.float32
    )
    log_total = jnp.log(jnp.sum(jnp.exp(logits_t), 0))
    target_hot = (alphabet[:, None] == tokens[None, :]).astype(jnp.float32)
    cross_ent = log_total - jnp.sum(target_hot * logits_t, 0)
    local_loss = jnp.sum(masked * cross_ent)
    probability = jnp.exp(logits_t - log_total[None, :])
    grad_logits = (
        masked[None, :] * (probability - target_hot) * (context_rows / mask_total)
    ).astype(jnp.bfloat16)
    head_part = lax.dot_general(
        grad_logits, head_weight, (((0,), (1,)), ((), ())), preferred_element_type=jnp.float32
    )
    grad_block = (head_part + grad_above.astype(jnp.float32)).astype(jnp.bfloat16)
    columns = tree_layout(grad_block, "seq")
    down_partial = lax.dot_general(
        columns, conv_act, (((0,), (0,)), ((), ())), preferred_element_type=jnp.float32
    )
    grad_conv_act = jnp.dot(grad_block, w_out, preferred_element_type=jnp.float32)
    gradient_before_activation = jax.vjp(norm_gelu, conv_pre)[1](grad_conv_act)[0].astype(
        jnp.bfloat16
    )
    back_pieces = spread(gradient_before_activation, shard_reach)
    backward_tap_pile = jnp.stack(back_pieces[::-1])
    grad_neck = jnp.einsum(
        "krc,kbc->rb", backward_tap_pile, conv_weight, preferred_element_type=jnp.float32
    )
    grad_first = jax.vjp(norm_gelu, first_pre)[1](grad_neck)[0].astype(jnp.bfloat16)
    columns = tree_layout(first_act, "seq")
    up_partial = lax.dot_general(
        columns, grad_first, (((0,), (0,)), ((), ())), preferred_element_type=jnp.float32
    )
    (grad_down, grad_up), loss_tile = tree_scatter(
        (down_partial, up_partial), jnp.broadcast_to(local_loss, (8, 128)), "seq"
    )
    grad_down = grad_down.astype(jnp.bfloat16)
    grad_up = grad_up.astype(jnp.bfloat16)
    loss_total = loss_tile[0, 0]
    return (loss_total / mask_total, grad_up, grad_down)


def solution(mesh):
    placed = (P("seq"), P("seq"), P("seq", None), P("seq", None), P(), P(), P(), P())
    return jax.shard_map(
        shards,
        mesh=mesh,
        in_specs=placed,
        out_specs=(P(), P("seq", None), P("seq", None)),
        check_vma=False,
    )
```

```python
import jax
import jax.numpy as jnp
from jax import lax
from jax.sharding import PartitionSpec as P


def from_behind(block, axis, distance):
    devices = range(lax.axis_size(axis))
    route = [(i - distance, i) for i in devices if i - distance in devices]
    return lax.ppermute(block, axis, route)


def swap_with(block, axis, bit):
    devices = lax.axis_size(axis)
    return lax.ppermute(block, axis, [(i, i ^ bit) for i in range(devices)])


def link_order(devices):
    bits = [1 << k for k in range(devices.bit_length() - 1)]
    near = [1, 2, 16, 64, 4, 32, 128, 8]
    return [b for b in near if b in bits] + [b for b in bits if b not in near]


def tree_sum(values, axis):
    for bit in link_order(lax.axis_size(axis)):
        values = values + swap_with(values, axis, bit)
    return values


def count_sum(counts, axis):
    order = link_order(lax.axis_size(axis))
    for first, second in zip(order[0::2], order[1::2]):
        counts = (
            counts
            + swap_with(counts, axis, first)
            + swap_with(counts, axis, second)
            + swap_with(counts, axis, first ^ second)
        )
    return counts


def tree_layout(columns, axis):
    devices = lax.axis_size(axis)
    depth = devices.bit_length() - 1
    rows, width = columns.shape
    split = columns.reshape((rows,) + (2,) * depth + (width // devices,))
    axes = [1 + depth - 1 - (bit.bit_length() - 1) for bit in link_order(devices)]
    return split.transpose([0] + axes + [depth + 1]).reshape(rows, width)


def tree_scatter(partials, extra, axis):
    devices = lax.axis_size(axis)
    me = lax.axis_index(axis)
    blocks = [p.reshape(devices, p.shape[0] // devices, -1) for p in partials]
    for bit in link_order(devices):
        half = blocks[0].shape[0] // 2
        upper = (me // bit) % 2
        keep = [lax.dynamic_slice_in_dim(b, upper * half, half, 0) for b in blocks]
        send = [
            lax.dynamic_slice_in_dim(b, (1 - upper) * half, half, 0).astype(jnp.bfloat16)
            for b in blocks
        ]
        pieces = 2 if half >= 16 else 1
        parts = [jnp.split(s, pieces, 0) for s in send]
        got_parts, got_extra = swap_with((parts, extra), axis, bit)
        got = [jnp.concatenate(g, 0) if pieces > 1 else g[0] for g in got_parts]
        blocks = [k + g.astype(jnp.float32) for k, g in zip(keep, got)]
        if extra is not None:
            extra = extra + got_extra
    return [b[0] for b in blocks], extra


def norm_gelu(values):
    centered = values - jnp.mean(values, -1, keepdims=True)
    variance = jnp.mean(centered * centered, -1, keepdims=True)
    return jax.nn.gelu(centered * lax.rsqrt(variance + 1e-05))


def spread(source_field, shard_reach):
    near_pieces = {}
    far_pieces = {}
    for direction in (1, -1):
        near_pieces[direction] = from_behind(source_field, "seq", direction * shard_reach)
    for direction in (1, -1):
        far_pieces[direction] = from_behind(source_field, "seq", 2 * direction * shard_reach)
    return [far_pieces[1], near_pieces[1], source_field, near_pieces[-1], far_pieces[-1]]


def shards(tokens, mask_flags, hidden_in, grad_above, w_in, conv_weight, w_out, head_weight):
    local_rows = tokens.shape[0]
    vocab_size = head_weight.shape[1]
    seq_devices = lax.axis_size("seq")
    shard_reach = 4
    context_rows = float(local_rows * seq_devices)
    masked = mask_flags.astype(jnp.float32)
    local_count = jnp.sum(masked)
    count_tile = tree_sum(jnp.broadcast_to(local_count, (8, 128)), "seq")
    alphabet = jnp.arange(vocab_size, dtype=jnp.int32)
    first_act = norm_gelu(hidden_in.astype(jnp.float32)).astype(jnp.bfloat16)
    first_pre = jnp.dot(first_act, w_in, preferred_element_type=jnp.float32)
    narrow_activation = norm_gelu(first_pre).astype(jnp.bfloat16)
    kernel_tap_pile = jnp.stack(spread(narrow_activation, shard_reach))
    count_tile, kernel_tap_pile = lax.optimization_barrier((count_tile, kernel_tap_pile))
    mask_total = count_tile[0, 0]
    conv_pre = jnp.einsum(
        "krc,kcb->rb", kernel_tap_pile, conv_weight, preferred_element_type=jnp.float32
    )
    conv_act = norm_gelu(conv_pre).astype(jnp.bfloat16)
    projected = lax.dot_general(
        conv_act, w_out, (((1,), (1,)), ((), ())), preferred_element_type=jnp.float32
    )
    block_out = (hidden_in.astype(jnp.float32) + projected).astype(jnp.bfloat16)
    logits_t = lax.dot_general(
        head_weight, block_out, (((0,), (1,)), ((), ())), preferred_element_type=jnp.float32
    )
    log_total = jnp.log(jnp.sum(jnp.exp(logits_t), 0))
    target_hot = (alphabet[:, None] == tokens[None, :]).astype(jnp.float32)
    cross_ent = log_total - jnp.sum(target_hot * logits_t, 0)
    local_loss = jnp.sum(masked * cross_ent)
    probability = jnp.exp(logits_t - log_total[None, :])
    grad_logits = (
        masked[None, :] * (probability - target_hot) * (context_rows / mask_total)
    ).astype(jnp.bfloat16)
    head_part = lax.dot_general(
        grad_logits, head_weight, (((0,), (1,)), ((), ())), preferred_element_type=jnp.float32
    )
    grad_block = (head_part + grad_above.astype(jnp.float32)).astype(jnp.bfloat16)
    columns = tree_layout(grad_block, "seq")
    down_partial = lax.dot_general(
        columns, conv_act, (((0,), (0,)), ((), ())), preferred_element_type=jnp.float32
    )
    grad_conv_act = jnp.dot(grad_block, w_out, preferred_element_type=jnp.float32)
    gradient_before_activation = jax.vjp(norm_gelu, conv_pre)[1](grad_conv_act)[0].astype(
        jnp.bfloat16
    )
    back_pieces = spread(gradient_before_activation, shard_reach)
    backward_tap_pile = jnp.stack(back_pieces[::-1])
    loss_tile = tree_sum(jnp.broadcast_to(local_loss, (8, 128)), "seq")
    loss_tile, backward_tap_pile = lax.optimization_barrier((loss_tile, backward_tap_pile))
    grad_neck = jnp.einsum(
        "krc,kbc->rb", backward_tap_pile, conv_weight, preferred_element_type=jnp.float32
    )
    grad_first = jax.vjp(norm_gelu, first_pre)[1](grad_neck)[0].astype(jnp.bfloat16)
    columns = tree_layout(first_act, "seq")
    up_partial = lax.dot_general(
        columns, grad_first, (((0,), (0,)), ((), ())), preferred_element_type=jnp.float32
    )
    (grad_down, grad_up), _ = tree_scatter((down_partial, up_partial), None, "seq")
    grad_down = grad_down.astype(jnp.bfloat16)
    grad_up = grad_up.astype(jnp.bfloat16)
    loss_total = loss_tile[0, 0]
    return (loss_total / mask_total, grad_up, grad_down)


def solution(mesh):
    placed = (P("seq"), P("seq"), P("seq", None), P("seq", None), P(), P(), P(), P())
    return jax.shard_map(
        shards,
        mesh=mesh,
        in_specs=placed,
        out_specs=(P(), P("seq", None), P("seq", None)),
        check_vma=False,
    )
```

```python
import jax
import jax.numpy as jnp
from jax import lax
from jax.sharding import PartitionSpec as P


def from_behind(block, axis, distance):
    devices = range(lax.axis_size(axis))
    route = [(i - distance, i) for i in devices if i - distance in devices]
    return lax.ppermute(block, axis, route)


def swap_with(block, axis, bit):
    devices = lax.axis_size(axis)
    return lax.ppermute(block, axis, [(i, i ^ bit) for i in range(devices)])


def link_order(devices):
    bits = [1 << k for k in range(devices.bit_length() - 1)]
    near = [1, 2, 16, 64, 4, 32, 128, 8]
    return [b for b in near if b in bits] + [b for b in bits if b not in near]


def tree_sum(values, axis):
    for bit in link_order(lax.axis_size(axis)):
        values = values + swap_with(values, axis, bit)
    return values


def count_sum(counts, axis):
    order = link_order(lax.axis_size(axis))
    for first, second in zip(order[0::2], order[1::2]):
        counts = (
            counts
            + swap_with(counts, axis, first)
            + swap_with(counts, axis, second)
            + swap_with(counts, axis, first ^ second)
        )
    return counts


def tree_layout(columns, axis):
    devices = lax.axis_size(axis)
    depth = devices.bit_length() - 1
    rows, width = columns.shape
    split = columns.reshape((rows,) + (2,) * depth + (width // devices,))
    axes = [1 + depth - 1 - (bit.bit_length() - 1) for bit in link_order(devices)]
    return split.transpose([0] + axes + [depth + 1]).reshape(rows, width)


def tree_scatter(partials, extra, axis):
    devices = lax.axis_size(axis)
    me = lax.axis_index(axis)
    blocks = [p.reshape(devices, p.shape[0] // devices, -1) for p in partials]
    for bit in link_order(devices):
        half = blocks[0].shape[0] // 2
        upper = (me // bit) % 2
        keep = [lax.dynamic_slice_in_dim(b, upper * half, half, 0) for b in blocks]
        send = [
            lax.dynamic_slice_in_dim(b, (1 - upper) * half, half, 0).astype(jnp.bfloat16)
            for b in blocks
        ]
        pieces = 2 if half >= 32 else 1
        parts = [jnp.split(s, pieces, 0) for s in send]
        got_parts, got_extra = swap_with((parts, extra), axis, bit)
        got = [jnp.concatenate(g, 0) if pieces > 1 else g[0] for g in got_parts]
        blocks = [k + g.astype(jnp.float32) for k, g in zip(keep, got)]
        extra = extra + got_extra
    return [b[0] for b in blocks], extra


def norm_gelu(values):
    centered = values - jnp.mean(values, -1, keepdims=True)
    variance = jnp.mean(centered * centered, -1, keepdims=True)
    return jax.nn.gelu(centered * lax.rsqrt(variance + 1e-05))


def spread(source_field, shard_reach):
    near_pieces = {}
    far_pieces = {}
    for direction in (1, -1):
        near_pieces[direction] = from_behind(source_field, "seq", direction * shard_reach)
    for direction in (1, -1):
        far_pieces[direction] = from_behind(source_field, "seq", 2 * direction * shard_reach)
    return [far_pieces[1], near_pieces[1], source_field, near_pieces[-1], far_pieces[-1]]


def shards(tokens, mask_flags, hidden_in, grad_above, w_in, conv_weight, w_out, head_weight):
    local_rows = tokens.shape[0]
    vocab_size = head_weight.shape[1]
    seq_devices = lax.axis_size("seq")
    shard_reach = 4
    context_rows = float(local_rows * seq_devices)
    masked = mask_flags.astype(jnp.float32)
    local_count = jnp.sum(masked)
    count_tile = tree_sum(jnp.broadcast_to(local_count, (8, 128)), "seq")
    alphabet = jnp.arange(vocab_size, dtype=jnp.int32)
    first_act = norm_gelu(hidden_in.astype(jnp.float32)).astype(jnp.bfloat16)
    first_pre = jnp.dot(first_act, w_in, preferred_element_type=jnp.float32)
    narrow_activation = norm_gelu(first_pre).astype(jnp.bfloat16)
    kernel_tap_pile = jnp.stack(spread(narrow_activation, shard_reach))
    count_tile, kernel_tap_pile = lax.optimization_barrier((count_tile, kernel_tap_pile))
    mask_total = count_tile[0, 0]
    conv_pre = jnp.einsum(
        "krc,kcb->rb", kernel_tap_pile, conv_weight, preferred_element_type=jnp.float32
    )
    conv_act = norm_gelu(conv_pre).astype(jnp.bfloat16)
    projected = lax.dot_general(
        conv_act, w_out, (((1,), (1,)), ((), ())), preferred_element_type=jnp.float32
    )
    block_out = (hidden_in.astype(jnp.float32) + projected).astype(jnp.bfloat16)
    logits_t = lax.dot_general(
        head_weight, block_out, (((0,), (1,)), ((), ())), preferred_element_type=jnp.float32
    )
    log_total = jnp.log(jnp.sum(jnp.exp(logits_t), 0))
    target_hot = (alphabet[:, None] == tokens[None, :]).astype(jnp.float32)
    cross_ent = log_total - jnp.sum(target_hot * logits_t, 0)
    local_loss = jnp.sum(masked * cross_ent)
    probability = jnp.exp(logits_t - log_total[None, :])
    grad_logits = (
        masked[None, :] * (probability - target_hot) * (context_rows / mask_total)
    ).astype(jnp.bfloat16)
    head_part = lax.dot_general(
        grad_logits, head_weight, (((0,), (1,)), ((), ())), preferred_element_type=jnp.float32
    )
    grad_block = (head_part + grad_above.astype(jnp.float32)).astype(jnp.bfloat16)
    columns = tree_layout(grad_block, "seq")
    down_partial = lax.dot_general(
        columns, conv_act, (((0,), (0,)), ((), ())), preferred_element_type=jnp.float32
    )
    grad_conv_act = jnp.dot(grad_block, w_out, preferred_element_type=jnp.float32)
    gradient_before_activation = jax.vjp(norm_gelu, conv_pre)[1](grad_conv_act)[0].astype(
        jnp.bfloat16
    )
    back_pieces = spread(gradient_before_activation, shard_reach)
    backward_tap_pile = jnp.stack(back_pieces[::-1])
    grad_neck = jnp.einsum(
        "krc,kbc->rb", backward_tap_pile, conv_weight, preferred_element_type=jnp.float32
    )
    grad_first = jax.vjp(norm_gelu, first_pre)[1](grad_neck)[0].astype(jnp.bfloat16)
    columns = tree_layout(first_act, "seq")
    up_partial = lax.dot_general(
        columns, grad_first, (((0,), (0,)), ((), ())), preferred_element_type=jnp.float32
    )
    (grad_down, grad_up), loss_tile = tree_scatter(
        (down_partial, up_partial), jnp.broadcast_to(local_loss, (8, 128)), "seq"
    )
    grad_down = grad_down.astype(jnp.bfloat16)
    grad_up = grad_up.astype(jnp.bfloat16)
    loss_total = loss_tile[0, 0]
    return (loss_total / mask_total, grad_up, grad_down)


def solution(mesh):
    placed = (P("seq"), P("seq"), P("seq", None), P("seq", None), P(), P(), P(), P())
    return jax.shard_map(
        shards,
        mesh=mesh,
        in_specs=placed,
        out_specs=(P(), P("seq", None), P("seq", None)),
        check_vma=False,
    )
```

```python
import jax
import jax.numpy as jnp
from jax import lax
from jax.sharding import PartitionSpec as P


def from_behind(block, axis, distance):
    devices = range(lax.axis_size(axis))
    route = [(i - distance, i) for i in devices if i - distance in devices]
    return lax.ppermute(block, axis, route)


def swap_with(block, axis, bit):
    devices = lax.axis_size(axis)
    return lax.ppermute(block, axis, [(i, i ^ bit) for i in range(devices)])


def link_order(devices):
    bits = [1 << k for k in range(devices.bit_length() - 1)]
    near = [1, 2, 16, 64, 4, 32, 128, 8]
    return [b for b in near if b in bits] + [b for b in bits if b not in near]


def tree_sum(values, axis):
    for bit in link_order(lax.axis_size(axis)):
        values = values + swap_with(values, axis, bit)
    return values


def count_sum(counts, axis):
    order = link_order(lax.axis_size(axis))
    for first, second in zip(order[0::2], order[1::2]):
        counts = (
            counts
            + swap_with(counts, axis, first)
            + swap_with(counts, axis, second)
            + swap_with(counts, axis, first ^ second)
        )
    return counts


def tree_layout(columns, axis):
    devices = lax.axis_size(axis)
    depth = devices.bit_length() - 1
    rows, width = columns.shape
    split = columns.reshape((rows,) + (2,) * depth + (width // devices,))
    axes = [1 + depth - 1 - (bit.bit_length() - 1) for bit in link_order(devices)]
    return split.transpose([0] + axes + [depth + 1]).reshape(rows, width)


def tree_scatter(partials, extra, axis):
    devices = lax.axis_size(axis)
    me = lax.axis_index(axis)
    blocks = [p.reshape(devices, p.shape[0] // devices, -1) for p in partials]
    for bit in link_order(devices):
        half = blocks[0].shape[0] // 2
        upper = (me // bit) % 2
        keep = [lax.dynamic_slice_in_dim(b, upper * half, half, 0) for b in blocks]
        send = [
            lax.dynamic_slice_in_dim(b, (1 - upper) * half, half, 0).astype(jnp.bfloat16)
            for b in blocks
        ]
        pieces = 2 if half >= 64 else 1
        parts = [jnp.split(s, pieces, 0) for s in send]
        got_parts, got_extra = swap_with((parts, extra), axis, bit)
        got = [jnp.concatenate(g, 0) if pieces > 1 else g[0] for g in got_parts]
        blocks = [k + g.astype(jnp.float32) for k, g in zip(keep, got)]
        extra = extra + got_extra
    return [b[0] for b in blocks], extra


def norm_gelu(values):
    centered = values - jnp.mean(values, -1, keepdims=True)
    variance = jnp.mean(centered * centered, -1, keepdims=True)
    return jax.nn.gelu(centered * lax.rsqrt(variance + 1e-05))


def spread(source_field, shard_reach):
    near_pieces = {}
    far_pieces = {}
    for direction in (1, -1):
        near_pieces[direction] = from_behind(source_field, "seq", direction * shard_reach)
    for direction in (1, -1):
        far_pieces[direction] = from_behind(source_field, "seq", 2 * direction * shard_reach)
    return [far_pieces[1], near_pieces[1], source_field, near_pieces[-1], far_pieces[-1]]


def shards(tokens, mask_flags, hidden_in, grad_above, w_in, conv_weight, w_out, head_weight):
    local_rows = tokens.shape[0]
    vocab_size = head_weight.shape[1]
    seq_devices = lax.axis_size("seq")
    shard_reach = 4
    context_rows = float(local_rows * seq_devices)
    masked = mask_flags.astype(jnp.float32)
    local_count = jnp.sum(masked)
    count_tile = tree_sum(jnp.broadcast_to(local_count, (8, 128)), "seq")
    alphabet = jnp.arange(vocab_size, dtype=jnp.int32)
    first_act = norm_gelu(hidden_in.astype(jnp.float32)).astype(jnp.bfloat16)
    first_pre = jnp.dot(first_act, w_in, preferred_element_type=jnp.float32)
    narrow_activation = norm_gelu(first_pre).astype(jnp.bfloat16)
    kernel_tap_pile = jnp.stack(spread(narrow_activation, shard_reach))
    count_tile, kernel_tap_pile = lax.optimization_barrier((count_tile, kernel_tap_pile))
    mask_total = count_tile[0, 0]
    conv_pre = jnp.einsum(
        "krc,kcb->rb", kernel_tap_pile, conv_weight, preferred_element_type=jnp.float32
    )
    conv_act = norm_gelu(conv_pre).astype(jnp.bfloat16)
    projected = lax.dot_general(
        conv_act, w_out, (((1,), (1,)), ((), ())), preferred_element_type=jnp.float32
    )
    block_out = (hidden_in.astype(jnp.float32) + projected).astype(jnp.bfloat16)
    logits_t = lax.dot_general(
        head_weight, block_out, (((0,), (1,)), ((), ())), preferred_element_type=jnp.float32
    )
    log_total = jnp.log(jnp.sum(jnp.exp(logits_t), 0))
    target_hot = (alphabet[:, None] == tokens[None, :]).astype(jnp.float32)
    cross_ent = log_total - jnp.sum(target_hot * logits_t, 0)
    local_loss = jnp.sum(masked * cross_ent)
    probability = jnp.exp(logits_t - log_total[None, :])
    grad_logits = (
        masked[None, :] * (probability - target_hot) * (context_rows / mask_total)
    ).astype(jnp.bfloat16)
    head_part = lax.dot_general(
        grad_logits, head_weight, (((0,), (1,)), ((), ())), preferred_element_type=jnp.float32
    )
    grad_block = (head_part + grad_above.astype(jnp.float32)).astype(jnp.bfloat16)
    columns = tree_layout(grad_block, "seq")
    down_partial = lax.dot_general(
        columns, conv_act, (((0,), (0,)), ((), ())), preferred_element_type=jnp.float32
    )
    grad_conv_act = jnp.dot(grad_block, w_out, preferred_element_type=jnp.float32)
    gradient_before_activation = jax.vjp(norm_gelu, conv_pre)[1](grad_conv_act)[0].astype(
        jnp.bfloat16
    )
    back_pieces = spread(gradient_before_activation, shard_reach)
    backward_tap_pile = jnp.stack(back_pieces[::-1])
    grad_neck = jnp.einsum(
        "krc,kbc->rb", backward_tap_pile, conv_weight, preferred_element_type=jnp.float32
    )
    grad_first = jax.vjp(norm_gelu, first_pre)[1](grad_neck)[0].astype(jnp.bfloat16)
    columns = tree_layout(first_act, "seq")
    up_partial = lax.dot_general(
        columns, grad_first, (((0,), (0,)), ((), ())), preferred_element_type=jnp.float32
    )
    (grad_down, grad_up), loss_tile = tree_scatter(
        (down_partial, up_partial), jnp.broadcast_to(local_loss, (8, 128)), "seq"
    )
    grad_down = grad_down.astype(jnp.bfloat16)
    grad_up = grad_up.astype(jnp.bfloat16)
    loss_total = loss_tile[0, 0]
    return (loss_total / mask_total, grad_up, grad_down)


def solution(mesh):
    placed = (P("seq"), P("seq"), P("seq", None), P("seq", None), P(), P(), P(), P())
    return jax.shard_map(
        shards,
        mesh=mesh,
        in_specs=placed,
        out_specs=(P(), P("seq", None), P("seq", None)),
        check_vma=False,
    )
```
